256 devices in a mesh: dp: 8 (over x, core), ctx: 32 (over z, y).
Axes of the slice: x: 4, y: 4, z: 8, core: 2. Of those that a mesh axis runs over, the one named last changes fastest.
Arguments:
- features: bfloat16 [8, 8192, 2560], P('dp', 'ctx'), may hold values from -5 to 5
- step_logits: float32 [8, 40, 8192], P('dp', None, 'ctx'), may hold values from -4 to 4
- writer: bfloat16 [8, 8192, 128], P('dp', 'ctx'), may hold values from -5 to 5
- reader: bfloat16 [8, 8192, 128], P('dp', 'ctx'), may hold values from -5 to 5
- log_rates: float32 [40], replicated, may hold values from -3 to 1
- step_bias: float32 [40], replicated, may hold values from -7 to -2
- skip_gain: float32 [40], replicated, may hold values from 0.5 to 1.5
- document_lengths: int32 [8, 4], P('dp'), may hold values from 1 to 4096, 8192 in all within a row
- cotangent: bfloat16 [8, 8192, 2560], P('dp', 'ctx'), may hold values from -5 to 5
Outputs:
- features_gradient: bfloat16 [8, 8192, 2560], P('dp', 'ctx')
- steps_gradient: float32 [8, 40, 8192], P('dp', None, 'ctx')
- writer_gradient: float32 [8, 8192, 128], P('dp', 'ctx')
- reader_gradient: float32 [8, 8192, 128], P('dp', 'ctx')
- head_gradient: float32 [3, 40], replicated
The draws below stay inside these ranges and needn't reach their ends.
Inputs may be any that keep to these rules, and one draw needn't show every extreme that they name: `document_lengths`: each row holds the lengths of 4 documents that sum to 8192; the longest of each row is exactly 4096.
All inputs are finite; a program needn't handle non-finite values.
Results may differ from the reference program's by a relative error of at most 0.001.
Values sent between devices are 32-bit elements; how exact they have to be, the bound alone decides.
No kernel may reach another device: no remote copies, remote signals or barrier semaphores. Data moves between devices by JAX's collectives and lax.ppermute only.
A program may use at most 256 MiB of HBM per device.

```python
import math
import jax
import jax.numpy as jnp
import numpy as np
from jax import lax

H = 40
P_SIZE = 64
N = 128
GROUP = 128
DOCS = 4
LENGTH = 8192
SEQS = 8


def block_levels(rng, extent, shards, low, high):
    def one(position, blocks):
        heights = jax.random.uniform(jax.random.fold_in(jax.random.fold_in(rng, 6), position), (blocks,), jnp.float32, low / len(shards), high / len(shards))
        return jnp.repeat(jnp.exp(heights), extent[position] // blocks).reshape((-1,) + (1,) * (len(extent) - position - 1))

    level = one(*shards[0])
    for cut in shards[1:]:
        level = level * one(*cut)
    return level


def profile(amount, total, most, lean):
    portions = [(1 << 20) // math.isqrt(standing ** lean) + 1 for standing in range(2, amount + 1)]
    rest, given = total - most - (amount - 1), [1] * (amount - 1)
    while rest > 0:
        candidates = [i for i in range(amount - 1) if given[i] < most]
        pool, left = sum([portions[i] for i in candidates]), rest
        for i in candidates:
            extra = min(most - given[i], max(1, left * portions[i] // pool), rest)
            given[i] = given[i] + extra
            rest = rest - extra
    return np.array([most] + given)


def ragged(own_key, amount, total, bound, slope):
    if amount == 2:
        one = jax.random.randint(own_key, (), max(1, total - bound), min(bound, total - 1) + 1)
        return jnp.stack([one, total - one])
    tallies = jnp.asarray(profile(amount, total, bound, slope), jnp.int32)
    pairs = (amount - 1) // 2
    giver, sink = tallies[1:1 + 2 * pairs:2], tallies[2:2 + 2 * pairs:2]
    slack = jnp.minimum(giver - 1, bound - sink)
    passed = jax.random.randint(jax.random.fold_in(own_key, 1), (pairs,), 0, 1 << 20) % (slack + 1)
    tallies = tallies.at[1:1 + 2 * pairs:2].set(giver - passed).at[2:2 + 2 * pairs:2].set(sink + passed)
    return tallies[jax.random.permutation(jax.random.fold_in(own_key, 2), amount)]


def noise(key, dims, deviation, bound, cuts=(), held_as=jnp.bfloat16):
    drawn = jax.random.normal(key, dims, jnp.float32) * deviation
    if len(cuts) > 0:
        drawn = block_levels(key, dims, cuts, -0.22, 0.18) * drawn
    return jnp.clip(drawn, min=-bound, max=bound).astype(held_as)


def setup_inputs(seed: int = 0) -> dict:
    streams_of = jax.random.split(jax.random.key(seed), 10)
    features = noise(streams_of[0], (SEQS, LENGTH, H * P_SIZE), 1.0, 5.0, ((0, 8), (1, 32)))
    step_logits = noise(streams_of[1], (SEQS, H, LENGTH), 1.0, 4.0, ((0, 8), (2, 32)), jnp.float32)
    writer = noise(streams_of[2], (SEQS, LENGTH, N), 1.0, 5.0, ((0, 8), (1, 32)))
    reader = noise(streams_of[3], (SEQS, LENGTH, N), 1.0, 5.0, ((0, 8), (1, 32)))
    log_rates = jnp.clip(jax.random.uniform(streams_of[4], (H,), jnp.float32, -3.0, 1.0), -3.0, 1.0)
    step_bias = jnp.clip(jax.random.uniform(streams_of[5], (H,), jnp.float32, -7.0, -2.0), -7.0, -2.0)
    skip_gain = jnp.clip(jax.random.uniform(streams_of[6], (H,), jnp.float32, 0.5, 1.5), 0.5, 1.5)
    document_lengths = jax.vmap(lambda own: ragged(own, DOCS, LENGTH, LENGTH // 2, 1))(jax.random.split(streams_of[7], SEQS)).reshape((SEQS, DOCS)).astype(jnp.int32)
    cotangent = noise(streams_of[8], (SEQS, LENGTH, H * P_SIZE), 1.0, 5.0, ((0, 8), (1, 32)))
    return dict(features=features, step_logits=step_logits, writer=writer, reader=reader, log_rates=log_rates, step_bias=step_bias, skip_gain=skip_gain, document_lengths=document_lengths, cotangent=cotangent)


HIGH = lax.Precision.HIGHEST

def group_step(state, prior_segment, inputs, log_decay, step_size, writer_piece, reader_piece, segment_piece, skip_gain):
    size = inputs.shape[0]
    cumulative = jnp.cumsum(log_decay, axis=1)
    causal = jnp.arange(size)[:, None] >= jnp.arange(size)[None, :]
    within = causal & (segment_piece[:, None] == segment_piece[None, :])
    spread = cumulative[:, :, None] - cumulative[:, None, :]
    decay = jnp.where(within[None], jnp.exp(jnp.where(within[None], spread, 0.0)), 0.0)
    scores = jnp.dot(reader_piece, writer_piece.T, precision=HIGH)
    weights = decay * scores[None] * step_size[:, None, :]
    inner = jnp.einsum('hts,shp->thp', weights, inputs, precision=HIGH)
    carry_in = jnp.where((segment_piece == prior_segment)[None], jnp.exp(cumulative), 0.0)
    from_state = jnp.einsum('tn,nhp->thp', reader_piece, state, precision=HIGH) * carry_in.T[:, :, None]
    result = inner + from_state + skip_gain[None, :, None] * inputs
    to_end = jnp.where((segment_piece == segment_piece[-1])[None], jnp.exp(cumulative[:, -1:] - cumulative), 0.0) * step_size
    fresh = jnp.einsum('hs,sn,shp->nhp', to_end, writer_piece, inputs, precision=HIGH)
    new_state = carry_in[:, -1][None, :, None] * state + fresh
    return (result, new_state)

def sequence_grads(items, log_rates, step_bias, skip_gain):
    features, step_logits, writer, reader, lengths, cotangent = items
    starts = jnp.cumsum(lengths)[:-1]
    segment = lax.optimization_barrier(jnp.sum(jnp.arange(LENGTH, dtype=jnp.int32)[:, None] >= starts[None, :], axis=1)).astype(jnp.int32)
    blocks = LENGTH // GROUP

    def forward(inputs, logits, writer_full, reader_full, rates, bias, gain):
        step_size = jax.nn.softplus(logits + bias[:, None])
        log_decay = -jnp.exp(rates)[:, None] * step_size
        pieces = (inputs.reshape(blocks, GROUP, H, P_SIZE), log_decay.reshape(H, blocks, GROUP).transpose(1, 0, 2), step_size.reshape(H, blocks, GROUP).transpose(1, 0, 2), writer_full.reshape(blocks, GROUP, N), reader_full.reshape(blocks, GROUP, N), segment.reshape(blocks, GROUP))

        def advance(carry, piece):
            state, prior = carry
            result, new_state = group_step(state, prior, piece[0], piece[1], piece[2], piece[3], piece[4], piece[5], gain)
            return ((new_state, piece[5][-1]), result)
        start = (jnp.zeros((N, H, P_SIZE), jnp.float32), jnp.array(-1, jnp.int32))
        _, results = lax.scan(jax.checkpoint(advance), start, pieces)
        return results.reshape(LENGTH, H, P_SIZE)
    _, pullback = jax.vjp(forward, features.astype(jnp.float32).reshape(LENGTH, H, P_SIZE), step_logits, writer.astype(jnp.float32), reader.astype(jnp.float32), log_rates, step_bias, skip_gain)
    grads = pullback(cotangent.astype(jnp.float32).reshape(LENGTH, H, P_SIZE))
    heads = jnp.stack([grads[4], grads[5], grads[6]])
    return (grads[0].reshape(LENGTH, H * P_SIZE).astype(jnp.bfloat16), grads[1], grads[2], grads[3], heads)

def reference(features, step_logits, writer, reader, log_rates, step_bias, skip_gain, document_lengths, cotangent):

    def one_sequence(items):
        return sequence_grads(items, log_rates, step_bias, skip_gain)
    outs = lax.map(one_sequence, (features, step_logits, writer, reader, document_lengths, cotangent))
    factor = float(SEQS * LENGTH) ** (-0.5)
    heads = lax.optimization_barrier(jnp.sum(outs[4], axis=0)) * factor
    return (outs[0], outs[1], outs[2], outs[3], heads)
```

```python
import jax
import jax.numpy as jnp
from jax import lax
from jax.sharding import PartitionSpec as P

GROUP = 128


HIGH = lax.Precision.HIGHEST


def exchange_scan(through, local_state, local_pull, axis):
    count = lax.axis_size(axis)
    rows, width = local_state.shape
    heads = through.shape[0]
    part = rows // count
    decays = lax.all_gather(through, axis)
    decays = jnp.repeat(decays, width // heads, axis=1)
    both = jnp.stack([local_state, local_pull]).reshape(2, count, part, width)
    moved = lax.all_to_all(jnp.swapaxes(both, 0, 1), axis, 0, 0, tiled=True)
    factor = jnp.stack([decays, decays[::-1]], axis=1)
    terms = jnp.stack([moved[:, 0], moved[::-1, 1]], axis=1)

    def link(earlier, later):
        return (earlier[0] * later[0], later[0][:, :, None, :] * earlier[1] + later[1])

    inclusive = lax.associative_scan(link, (factor, terms), axis=0)[1]
    exclusive = jnp.concatenate([jnp.zeros_like(inclusive[:1]), inclusive[:-1]], axis=0)
    ordered = jnp.stack([exclusive[:, 0], exclusive[::-1, 1]], axis=1)
    back = lax.all_to_all(ordered, axis, 0, 0, tiled=True)
    joined = jnp.swapaxes(back, 0, 1).reshape(2, rows, width)
    return joined[0], joined[1]


def group_step(
    state,
    prior_segment,
    inputs,
    log_decay,
    step_size,
    scores,
    reader_piece,
    writer_piece,
    segment_piece,
    skip_gain,
):
    size = inputs.shape[0]
    cumulative = jnp.cumsum(log_decay, axis=1)
    causal = jnp.arange(size)[:, None] >= jnp.arange(size)[None, :]
    within = causal & (segment_piece[:, None] == segment_piece[None, :])
    spread = cumulative[:, :, None] - cumulative[:, None, :]
    decay = jnp.where(within[None], jnp.exp(jnp.where(within[None], spread, 0.0)), 0.0)
    weights = decay * scores[None] * step_size[:, None, :]
    inner = jnp.einsum("hts,shp->thp", weights, inputs, precision=HIGH)
    carry_in = jnp.where((segment_piece == prior_segment)[None], jnp.exp(cumulative), 0.0)
    from_state = (
        jnp.einsum("tn,nhp->thp", reader_piece, state, precision=HIGH) * carry_in.T[:, :, None]
    )
    result = inner + from_state + skip_gain[None, :, None] * inputs
    to_end = (
        jnp.where(
            (segment_piece == segment_piece[-1])[None],
            jnp.exp(cumulative[:, -1:] - cumulative),
            0.0,
        )
        * step_size
    )
    fresh = jnp.einsum("hs,sn,shp->nhp", to_end, writer_piece, inputs, precision=HIGH)
    new_state = carry_in[:, -1][None, :, None] * state + fresh
    return (result, new_state)


def shards(
    features,
    step_logits,
    writer,
    reader,
    log_rates,
    step_bias,
    skip_gain,
    document_lengths,
    cotangent,
):
    tokens = features.shape[1]
    width = features.shape[2]
    heads = log_rates.shape[0]
    head_size = width // heads
    state_rows = writer.shape[2]
    blocks = tokens // GROUP
    position = lax.axis_index("ctx") * tokens + jnp.arange(tokens, dtype=jnp.int32)
    starts = jnp.cumsum(document_lengths[0])[:-1]
    segment = jnp.sum(position[:, None] >= starts[None, :], axis=1)
    prior_segment = jnp.sum(position[0] - 1 >= starts)
    inputs = features[0].astype(jnp.float32).reshape(tokens, heads, head_size)
    writer_full = writer[0].astype(jnp.float32)
    reader_full = reader[0].astype(jnp.float32)
    upstream = cotangent[0].astype(jnp.float32).reshape(tokens, heads, head_size)
    all_scores = jnp.einsum(
        "ctn,csn->cts",
        reader[0].reshape(blocks, GROUP, state_rows),
        writer[0].reshape(blocks, GROUP, state_rows),
        preferred_element_type=jnp.float32,
    )
    step_size = jax.nn.softplus(step_logits[0] + step_bias[:, None])
    log_decay = -jnp.exp(log_rates)[:, None] * step_size
    cumulative = jnp.cumsum(log_decay, axis=1)
    from_start = jnp.where((segment == prior_segment)[None], jnp.exp(cumulative), 0.0)
    through = from_start[:, -1]
    to_end = (
        jnp.where((segment == segment[-1])[None], jnp.exp(cumulative[:, -1:] - cumulative), 0.0)
        * step_size
    )
    local_state = jnp.einsum("hs,sn,shp->nhp", to_end, writer_full, inputs, precision=HIGH).reshape(
        state_rows, width
    )
    local_pull = jnp.einsum(
        "ht,tn,thp->nhp", from_start, reader_full, upstream, precision=HIGH
    ).reshape(state_rows, width)
    start_state, end_pull = exchange_scan(through, local_state, local_pull, "ctx")
    stepper = jax.checkpoint(group_step)

    def forward(inputs_in, logits, writer_in, reader_in, scores_in, rates, bias, gain):
        sizes_in = jax.nn.softplus(logits + bias[:, None])
        decays_in = -jnp.exp(rates)[:, None] * sizes_in
        state = start_state.reshape(state_rows, heads, head_size)
        prior = prior_segment
        results = []
        for number in range(blocks):
            first = number * GROUP
            final = first + GROUP
            result, state = stepper(
                state,
                prior,
                inputs_in[first:final],
                decays_in[:, first:final],
                sizes_in[:, first:final],
                scores_in[number],
                reader_in[first:final],
                writer_in[first:final],
                segment[first:final],
                gain,
            )
            prior = segment[final - 1]
            results.append(result)
        return (jnp.concatenate(results, axis=0), state)

    _, pullback = jax.vjp(
        forward,
        inputs,
        step_logits[0],
        writer_full,
        reader_full,
        all_scores,
        log_rates,
        step_bias,
        skip_gain,
    )
    grads = pullback((upstream, end_pull.reshape(state_rows, heads, head_size)))
    score_grads = grads[4]
    reader_extra = jnp.einsum(
        "cts,csn->ctn", score_grads, writer_full.reshape(blocks, GROUP, state_rows), precision=HIGH
    ).reshape(tokens, state_rows)
    writer_extra = jnp.einsum(
        "cts,ctn->csn", score_grads, reader_full.reshape(blocks, GROUP, state_rows), precision=HIGH
    ).reshape(tokens, state_rows)
    factor = float(lax.axis_size("dp") * lax.axis_size("ctx") * tokens) ** (-0.5)
    head_terms = jnp.stack([grads[5], grads[6], grads[7]]) * factor
    head_total = lax.psum(head_terms, ("dp", "ctx"))
    features_gradient = grads[0].reshape(tokens, width).astype(jnp.bfloat16)[None]
    return (
        features_gradient,
        grads[1][None],
        (grads[2] + writer_extra)[None],
        (grads[3] + reader_extra)[None],
        head_total,
    )


def solution(mesh):
    placed = (
        P("dp", "ctx", None),
        P("dp", None, "ctx"),
        P("dp", "ctx", None),
        P("dp", "ctx", None),
        P(),
        P(),
        P(),
        P("dp", None),
        P("dp", "ctx", None),
    )
    return jax.shard_map(
        shards,
        mesh=mesh,
        in_specs=placed,
        out_specs=(
            P("dp", "ctx", None),
            P("dp", None, "ctx"),
            P("dp", "ctx", None),
            P("dp", "ctx", None),
            P(),
        ),
        check_vma=False,
    )
```

```python
import jax
import jax.numpy as jnp
from jax import lax
from jax.experimental import pallas as pl
from jax.sharding import PartitionSpec as P

GROUP = 128


HIGH = lax.Precision.HIGHEST


def scan_kernel(recv_ref, out_ref):
    count = recv_ref.shape[0]
    part = out_ref.shape[1] // 2
    zero = jnp.zeros((part, recv_ref.shape[2]), jnp.float32)

    def forward(j, state):
        out_ref[j, 0:part, :] = state
        return recv_ref[j, 2 * part : 2 * part + 1, :] * state + recv_ref[j, 0:part, :]

    def backward(k, pull):
        j = count - 1 - k
        out_ref[j, part : 2 * part, :] = pull
        return recv_ref[j, 2 * part : 2 * part + 1, :] * pull + recv_ref[j, part : 2 * part, :]

    lax.fori_loop(0, count, forward, zero)
    lax.fori_loop(0, count, backward, zero)


def exchange_scan(through, local_state, local_pull, axis):
    count = lax.axis_size(axis)
    rows, width = local_state.shape
    heads = through.shape[0]
    part = rows // count
    through_wide = jnp.broadcast_to(
        jnp.repeat(through, width // heads)[None, None, :], (count, 1, width)
    )
    sent = jnp.concatenate(
        [local_state.reshape(count, part, width), local_pull.reshape(count, part, width), through_wide],
        axis=1,
    )
    moved = lax.all_to_all(sent, axis, 0, 0, tiled=True)
    scanned = pl.pallas_call(
        scan_kernel,
        out_shape=jax.ShapeDtypeStruct((count, 2 * part, width), jnp.float32),
    )(moved)
    back = lax.all_to_all(scanned, axis, 0, 0, tiled=True)
    start_state = back[:, 0:part, :].reshape(rows, width)
    end_pull = back[:, part : 2 * part, :].reshape(rows, width)
    return start_state, end_pull


def group_step(
    state,
    prior_segment,
    inputs,
    log_decay,
    step_size,
    scores,
    reader_piece,
    writer_piece,
    segment_piece,
    skip_gain,
):
    size = inputs.shape[0]
    cumulative = jnp.cumsum(log_decay, axis=1)
    causal = jnp.arange(size)[:, None] >= jnp.arange(size)[None, :]
    within = causal & (segment_piece[:, None] == segment_piece[None, :])
    spread = cumulative[:, :, None] - cumulative[:, None, :]
    decay = jnp.where(within[None], jnp.exp(jnp.where(within[None], spread, 0.0)), 0.0)
    weights = decay * scores[None] * step_size[:, None, :]
    inner = jnp.einsum("hts,shp->thp", weights, inputs, precision=HIGH)
    carry_in = jnp.where((segment_piece == prior_segment)[None], jnp.exp(cumulative), 0.0)
    from_state = (
        jnp.einsum("tn,nhp->thp", reader_piece, state, precision=HIGH) * carry_in.T[:, :, None]
    )
    result = inner + from_state + skip_gain[None, :, None] * inputs
    to_end = (
        jnp.where(
            (segment_piece == segment_piece[-1])[None],
            jnp.exp(cumulative[:, -1:] - cumulative),
            0.0,
        )
        * step_size
    )
    fresh = jnp.einsum("hs,sn,shp->nhp", to_end, writer_piece, inputs, precision=HIGH)
    new_state = carry_in[:, -1][None, :, None] * state + fresh
    return (result, new_state)


def shards(
    features,
    step_logits,
    writer,
    reader,
    log_rates,
    step_bias,
    skip_gain,
    document_lengths,
    cotangent,
):
    tokens = features.shape[1]
    width = features.shape[2]
    heads = log_rates.shape[0]
    head_size = width // heads
    state_rows = writer.shape[2]
    blocks = tokens // GROUP
    position = lax.axis_index("ctx") * tokens + jnp.arange(tokens, dtype=jnp.int32)
    starts = jnp.cumsum(document_lengths[0])[:-1]
    segment = jnp.sum(position[:, None] >= starts[None, :], axis=1)
    prior_segment = jnp.sum(position[0] - 1 >= starts)
    inputs = features[0].astype(jnp.float32).reshape(tokens, heads, head_size)
    writer_full = writer[0].astype(jnp.float32)
    reader_full = reader[0].astype(jnp.float32)
    upstream = cotangent[0].astype(jnp.float32).reshape(tokens, heads, head_size)
    all_scores = jnp.einsum(
        "ctn,csn->cts",
        reader[0].reshape(blocks, GROUP, state_rows),
        writer[0].reshape(blocks, GROUP, state_rows),
        preferred_element_type=jnp.float32,
    )
    step_size = jax.nn.softplus(step_logits[0] + step_bias[:, None])
    log_decay = -jnp.exp(log_rates)[:, None] * step_size
    cumulative = jnp.cumsum(log_decay, axis=1)
    from_start = jnp.where((segment == prior_segment)[None], jnp.exp(cumulative), 0.0)
    through = from_start[:, -1]
    to_end = (
        jnp.where((segment == segment[-1])[None], jnp.exp(cumulative[:, -1:] - cumulative), 0.0)
        * step_size
    )
    local_state = jnp.einsum("hs,sn,shp->nhp", to_end, writer_full, inputs, precision=HIGH).reshape(
        state_rows, width
    )
    local_pull = jnp.einsum(
        "ht,tn,thp->nhp", from_start, reader_full, upstream, precision=HIGH
    ).reshape(state_rows, width)
    start_state, end_pull = exchange_scan(through, local_state, local_pull, "ctx")
    stepper = jax.checkpoint(group_step)

    def forward(inputs_in, logits, writer_in, reader_in, scores_in, rates, bias, gain):
        sizes_in = jax.nn.softplus(logits + bias[:, None])
        decays_in = -jnp.exp(rates)[:, None] * sizes_in
        state = start_state.reshape(state_rows, heads, head_size)
        prior = prior_segment
        results = []
        for number in range(blocks):
            first = number * GROUP
            final = first + GROUP
            result, state = stepper(
                state,
                prior,
                inputs_in[first:final],
                decays_in[:, first:final],
                sizes_in[:, first:final],
                scores_in[number],
                reader_in[first:final],
                writer_in[first:final],
                segment[first:final],
                gain,
            )
            prior = segment[final - 1]
            results.append(result)
        return (jnp.concatenate(results, axis=0), state)

    _, pullback = jax.vjp(
        forward,
        inputs,
        step_logits[0],
        writer_full,
        reader_full,
        all_scores,
        log_rates,
        step_bias,
        skip_gain,
    )
    grads = pullback((upstream, end_pull.reshape(state_rows, heads, head_size)))
    score_grads = grads[4]
    reader_extra = jnp.einsum(
        "cts,csn->ctn", score_grads, writer_full.reshape(blocks, GROUP, state_rows), precision=HIGH
    ).reshape(tokens, state_rows)
    writer_extra = jnp.einsum(
        "cts,ctn->csn", score_grads, reader_full.reshape(blocks, GROUP, state_rows), precision=HIGH
    ).reshape(tokens, state_rows)
    factor = float(lax.axis_size("dp") * lax.axis_size("ctx") * tokens) ** (-0.5)
    head_terms = jnp.stack([grads[5], grads[6], grads[7]]) * factor
    head_total = lax.psum(head_terms, ("dp", "ctx"))
    features_gradient = grads[0].reshape(tokens, width).astype(jnp.bfloat16)[None]
    return (
        features_gradient,
        grads[1][None],
        (grads[2] + writer_extra)[None],
        (grads[3] + reader_extra)[None],
        head_total,
    )


def solution(mesh):
    placed = (
        P("dp", "ctx", None),
        P("dp", None, "ctx"),
        P("dp", "ctx", None),
        P("dp", "ctx", None),
        P(),
        P(),
        P(),
        P("dp", None),
        P("dp", "ctx", None),
    )
    return jax.shard_map(
        shards,
        mesh=mesh,
        in_specs=placed,
        out_specs=(
            P("dp", "ctx", None),
            P("dp", None, "ctx"),
            P("dp", "ctx", None),
            P("dp", "ctx", None),
            P(),
        ),
        check_vma=False,
    )
```

```python
import jax
import jax.numpy as jnp
from jax import lax
from jax.experimental import pallas as pl
from jax.sharding import PartitionSpec as P

GROUP = 128


HIGH = lax.Precision.HIGHEST


def scan_kernel(state_ref, pull_ref, decay_ref, out_ref):
    count = state_ref.shape[0]
    part = state_ref.shape[1]
    zero = jnp.zeros((part, out_ref.shape[2]), jnp.float32)

    def forward(j, state):
        out_ref[j, 0:part, :] = state
        return decay_ref[j] * state + state_ref[j]

    def backward(k, pull):
        j = count - 1 - k
        out_ref[j, part : 2 * part, :] = pull
        return decay_ref[j] * pull + pull_ref[j]

    lax.fori_loop(0, count, forward, zero)
    lax.fori_loop(0, count, backward, zero)


def exchange_scan(through, local_state, local_pull, axis):
    count = lax.axis_size(axis)
    rows, width = local_state.shape
    heads = through.shape[0]
    part = rows // count
    spare = 128 * ((heads + 127) // 128)
    extra = jnp.zeros((count, part, spare), jnp.float32).at[:, 0, :heads].set(through[None, :])
    sent_state = jnp.concatenate([local_state.reshape(count, part, width), extra], axis=2)
    moved_state = lax.all_to_all(sent_state, axis, 0, 0, tiled=True)
    moved_pull = lax.all_to_all(local_pull.reshape(count, part, width), axis, 0, 0, tiled=True)
    decays = jnp.repeat(moved_state[:, 0, width : width + heads], width // heads, axis=1)[:, None, :]
    lanes = 512 if width % 512 == 0 else width
    scanned = pl.pallas_call(
        scan_kernel,
        out_shape=jax.ShapeDtypeStruct((count, 2 * part, width), jnp.float32),
        grid=(width // lanes,),
        in_specs=[
            pl.BlockSpec((count, part, lanes), lambda c: (0, 0, c)),
            pl.BlockSpec((count, part, lanes), lambda c: (0, 0, c)),
            pl.BlockSpec((count, 1, lanes), lambda c: (0, 0, c)),
        ],
        out_specs=pl.BlockSpec((count, 2 * part, lanes), lambda c: (0, 0, c)),
    )(moved_state, moved_pull, decays)
    back = lax.all_to_all(scanned, axis, 0, 0, tiled=True)
    start_state = back[:, 0:part, :].reshape(rows, width)
    end_pull = back[:, part : 2 * part, :].reshape(rows, width)
    return start_state, end_pull


def group_step(
    state,
    prior_segment,
    inputs,
    log_decay,
    step_size,
    scores,
    reader_piece,
    writer_piece,
    segment_piece,
    skip_gain,
):
    size = inputs.shape[0]
    cumulative = jnp.cumsum(log_decay, axis=1)
    causal = jnp.arange(size)[:, None] >= jnp.arange(size)[None, :]
    within = causal & (segment_piece[:, None] == segment_piece[None, :])
    spread = cumulative[:, :, None] - cumulative[:, None, :]
    decay = jnp.where(within[None], jnp.exp(jnp.where(within[None], spread, 0.0)), 0.0)
    weights = decay * scores[None] * step_size[:, None, :]
    inner = jnp.einsum("hts,shp->thp", weights, inputs, precision=HIGH)
    carry_in = jnp.where((segment_piece == prior_segment)[None], jnp.exp(cumulative), 0.0)
    from_state = (
        jnp.einsum("tn,nhp->thp", reader_piece, state, precision=HIGH) * carry_in.T[:, :, None]
    )
    result = inner + from_state + skip_gain[None, :, None] * inputs
    to_end = (
        jnp.where(
            (segment_piece == segment_piece[-1])[None],
            jnp.exp(cumulative[:, -1:] - cumulative),
            0.0,
        )
        * step_size
    )
    fresh = jnp.einsum("hs,sn,shp->nhp", to_end, writer_piece, inputs, precision=HIGH)
    new_state = carry_in[:, -1][None, :, None] * state + fresh
    return (result, new_state)


def shards(
    features,
    step_logits,
    writer,
    reader,
    log_rates,
    step_bias,
    skip_gain,
    document_lengths,
    cotangent,
):
    tokens = features.shape[1]
    width = features.shape[2]
    heads = log_rates.shape[0]
    head_size = width // heads
    state_rows = writer.shape[2]
    blocks = tokens // GROUP
    position = lax.axis_index("ctx") * tokens + jnp.arange(tokens, dtype=jnp.int32)
    starts = jnp.cumsum(document_lengths[0])[:-1]
    segment = jnp.sum(position[:, None] >= starts[None, :], axis=1)
    prior_segment = jnp.sum(position[0] - 1 >= starts)
    inputs = features[0].astype(jnp.float32).reshape(tokens, heads, head_size)
    writer_full = writer[0].astype(jnp.float32)
    reader_full = reader[0].astype(jnp.float32)
    upstream = cotangent[0].astype(jnp.float32).reshape(tokens, heads, head_size)
    all_scores = jnp.einsum(
        "ctn,csn->cts",
        reader[0].reshape(blocks, GROUP, state_rows),
        writer[0].reshape(blocks, GROUP, state_rows),
        preferred_element_type=jnp.float32,
    )
    step_size = jax.nn.softplus(step_logits[0] + step_bias[:, None])
    log_decay = -jnp.exp(log_rates)[:, None] * step_size
    cumulative = jnp.cumsum(log_decay, axis=1)
    from_start = jnp.where((segment == prior_segment)[None], jnp.exp(cumulative), 0.0)
    through = from_start[:, -1]
    to_end = (
        jnp.where((segment == segment[-1])[None], jnp.exp(cumulative[:, -1:] - cumulative), 0.0)
        * step_size
    )
    local_state = jnp.einsum("hs,sn,shp->nhp", to_end, writer_full, inputs, precision=HIGH).reshape(
        state_rows, width
    )
    local_pull = jnp.einsum(
        "ht,tn,thp->nhp", from_start, reader_full, upstream, precision=HIGH
    ).reshape(state_rows, width)
    start_state, end_pull = exchange_scan(through, local_state, local_pull, "ctx")
    stepper = jax.checkpoint(group_step)

    def forward(inputs_in, logits, writer_in, reader_in, scores_in, rates, bias, gain):
        sizes_in = jax.nn.softplus(logits + bias[:, None])
        decays_in = -jnp.exp(rates)[:, None] * sizes_in
        state = start_state.reshape(state_rows, heads, head_size)
        prior = prior_segment
        results = []
        for number in range(blocks):
            first = number * GROUP
            final = first + GROUP
            result, state = stepper(
                state,
                prior,
                inputs_in[first:final],
                decays_in[:, first:final],
                sizes_in[:, first:final],
                scores_in[number],
                reader_in[first:final],
                writer_in[first:final],
                segment[first:final],
                gain,
            )
            prior = segment[final - 1]
            results.append(result)
        return (jnp.concatenate(results, axis=0), state)

    _, pullback = jax.vjp(
        forward,
        inputs,
        step_logits[0],
        writer_full,
        reader_full,
        all_scores,
        log_rates,
        step_bias,
        skip_gain,
    )
    grads = pullback((upstream, end_pull.reshape(state_rows, heads, head_size)))
    score_grads = grads[4]
    reader_extra = jnp.einsum(
        "cts,csn->ctn", score_grads, writer_full.reshape(blocks, GROUP, state_rows), precision=HIGH
    ).reshape(tokens, state_rows)
    writer_extra = jnp.einsum(
        "cts,ctn->csn", score_grads, reader_full.reshape(blocks, GROUP, state_rows), precision=HIGH
    ).reshape(tokens, state_rows)
    factor = float(lax.axis_size("dp") * lax.axis_size("ctx") * tokens) ** (-0.5)
    head_terms = jnp.stack([grads[5], grads[6], grads[7]]) * factor
    head_total = jnp.sum(lax.all_gather(head_terms, ("dp", "ctx")), axis=0)
    features_gradient = grads[0].reshape(tokens, width).astype(jnp.bfloat16)[None]
    return (
        features_gradient,
        grads[1][None],
        (grads[2] + writer_extra)[None],
        (grads[3] + reader_extra)[None],
        head_total,
    )


def solution(mesh):
    placed = (
        P("dp", "ctx", None),
        P("dp", None, "ctx"),
        P("dp", "ctx", None),
        P("dp", "ctx", None),
        P(),
        P(),
        P(),
        P("dp", None),
        P("dp", "ctx", None),
    )
    return jax.shard_map(
        shards,
        mesh=mesh,
        in_specs=placed,
        out_specs=(
            P("dp", "ctx", None),
            P("dp", None, "ctx"),
            P("dp", "ctx", None),
            P("dp", "ctx", None),
            P(),
        ),
        check_vma=False,
    )
```

```python
import jax
import jax.numpy as jnp
from jax import lax
from jax.experimental import pallas as pl
from jax.sharding import PartitionSpec as P

GROUP = 128


HIGH = lax.Precision.HIGHEST


def scan_kernel(moved_ref, decay_ref, out_ref):
    count = moved_ref.shape[0]
    part = moved_ref.shape[1] // 2
    zero = jnp.zeros((part, out_ref.shape[2]), jnp.float32)

    def forward(j, state):
        out_ref[j, 0:part, :] = state
        return decay_ref[j] * state + moved_ref[j, 0:part, :]

    def backward(k, pull):
        j = count - 1 - k
        out_ref[j, part : 2 * part, :] = pull
        return decay_ref[j] * pull + moved_ref[j, part : 2 * part, :]

    lax.fori_loop(0, count, forward, zero)
    lax.fori_loop(0, count, backward, zero)


def exchange_scan(through, local_state, local_pull, axis):
    count = lax.axis_size(axis)
    rows, width = local_state.shape
    heads = through.shape[0]
    part = rows // count
    spare = 128 * ((heads + 127) // 128)
    extra = jnp.zeros((count, 1, spare), jnp.float32).at[:, 0, :heads].set(through[None, :])
    moved_decay = lax.all_to_all(extra, axis, 0, 0, tiled=True)
    sent = jnp.concatenate(
        [local_state.reshape(count, part, width), local_pull.reshape(count, part, width)], axis=1
    )
    moved = lax.all_to_all(sent, axis, 0, 0, tiled=True)
    decays = jnp.repeat(moved_decay[:, 0, :heads], width // heads, axis=1)[:, None, :]
    lanes = 512 if width % 512 == 0 else width
    scanned = pl.pallas_call(
        scan_kernel,
        out_shape=jax.ShapeDtypeStruct((count, 2 * part, width), jnp.float32),
        grid=(width // lanes,),
        in_specs=[
            pl.BlockSpec((count, 2 * part, lanes), lambda c: (0, 0, c)),
            pl.BlockSpec((count, 1, lanes), lambda c: (0, 0, c)),
        ],
        out_specs=pl.BlockSpec((count, 2 * part, lanes), lambda c: (0, 0, c)),
    )(moved, decays)
    back = lax.all_to_all(scanned, axis, 0, 0, tiled=True)
    start_state = back[:, 0:part, :].reshape(rows, width)
    end_pull = back[:, part : 2 * part, :].reshape(rows, width)
    return start_state, end_pull


def group_step(
    state,
    prior_segment,
    inputs,
    log_decay,
    step_size,
    scores,
    reader_piece,
    writer_piece,
    segment_piece,
    skip_gain,
):
    size = inputs.shape[0]
    cumulative = jnp.cumsum(log_decay, axis=1)
    causal = jnp.arange(size)[:, None] >= jnp.arange(size)[None, :]
    within = causal & (segment_piece[:, None] == segment_piece[None, :])
    spread = cumulative[:, :, None] - cumulative[:, None, :]
    decay = jnp.where(within[None], jnp.exp(jnp.where(within[None], spread, 0.0)), 0.0)
    weights = decay * scores[None] * step_size[:, None, :]
    inner = jnp.einsum("hts,shp->thp", weights, inputs, precision=HIGH)
    carry_in = jnp.where((segment_piece == prior_segment)[None], jnp.exp(cumulative), 0.0)
    from_state = (
        jnp.einsum("tn,nhp->thp", reader_piece, state, precision=HIGH) * carry_in.T[:, :, None]
    )
    result = inner + from_state + skip_gain[None, :, None] * inputs
    to_end = (
        jnp.where(
            (segment_piece == segment_piece[-1])[None],
            jnp.exp(cumulative[:, -1:] - cumulative),
            0.0,
        )
        * step_size
    )
    fresh = jnp.einsum("hs,sn,shp->nhp", to_end, writer_piece, inputs, precision=HIGH)
    new_state = carry_in[:, -1][None, :, None] * state + fresh
    return (result, new_state)


def shards(
    features,
    step_logits,
    writer,
    reader,
    log_rates,
    step_bias,
    skip_gain,
    document_lengths,
    cotangent,
):
    tokens = features.shape[1]
    width = features.shape[2]
    heads = log_rates.shape[0]
    head_size = width // heads
    state_rows = writer.shape[2]
    blocks = tokens // GROUP
    position = lax.axis_index("ctx") * tokens + jnp.arange(tokens, dtype=jnp.int32)
    starts = jnp.cumsum(document_lengths[0])[:-1]
    segment = jnp.sum(position[:, None] >= starts[None, :], axis=1)
    prior_segment = jnp.sum(position[0] - 1 >= starts)
    inputs = features[0].astype(jnp.float32).reshape(tokens, heads, head_size)
    writer_full = writer[0].astype(jnp.float32)
    reader_full = reader[0].astype(jnp.float32)
    upstream = cotangent[0].astype(jnp.float32).reshape(tokens, heads, head_size)
    all_scores = jnp.einsum(
        "ctn,csn->cts",
        reader[0].reshape(blocks, GROUP, state_rows),
        writer[0].reshape(blocks, GROUP, state_rows),
        preferred_element_type=jnp.float32,
    )
    step_size = jax.nn.softplus(step_logits[0] + step_bias[:, None])
    log_decay = -jnp.exp(log_rates)[:, None] * step_size
    cumulative = jnp.cumsum(log_decay, axis=1)
    from_start = jnp.where((segment == prior_segment)[None], jnp.exp(cumulative), 0.0)
    through = from_start[:, -1]
    to_end = (
        jnp.where((segment == segment[-1])[None], jnp.exp(cumulative[:, -1:] - cumulative), 0.0)
        * step_size
    )
    local_state = jnp.einsum("hs,sn,shp->nhp", to_end, writer_full, inputs, precision=HIGH).reshape(
        state_rows, width
    )
    local_pull = jnp.einsum(
        "ht,tn,thp->nhp", from_start, reader_full, upstream, precision=HIGH
    ).reshape(state_rows, width)
    start_state, end_pull = exchange_scan(through, local_state, local_pull, "ctx")
    stepper = jax.checkpoint(group_step)

    def forward(inputs_in, logits, writer_in, reader_in, scores_in, rates, bias, gain):
        sizes_in = jax.nn.softplus(logits + bias[:, None])
        decays_in = -jnp.exp(rates)[:, None] * sizes_in
        state = start_state.reshape(state_rows, heads, head_size)
        prior = prior_segment
        results = []
        for number in range(blocks):
            first = number * GROUP
            final = first + GROUP
            result, state = stepper(
                state,
                prior,
                inputs_in[first:final],
                decays_in[:, first:final],
                sizes_in[:, first:final],
                scores_in[number],
                reader_in[first:final],
                writer_in[first:final],
                segment[first:final],
                gain,
            )
            prior = segment[final - 1]
            results.append(result)
        return (jnp.concatenate(results, axis=0), state)

    _, pullback = jax.vjp(
        forward,
        inputs,
        step_logits[0],
        writer_full,
        reader_full,
        all_scores,
        log_rates,
        step_bias,
        skip_gain,
    )
    grads = pullback((upstream, end_pull.reshape(state_rows, heads, head_size)))
    score_grads = grads[4]
    reader_extra = jnp.einsum(
        "cts,csn->ctn", score_grads, writer_full.reshape(blocks, GROUP, state_rows), precision=HIGH
    ).reshape(tokens, state_rows)
    writer_extra = jnp.einsum(
        "cts,ctn->csn", score_grads, reader_full.reshape(blocks, GROUP, state_rows), precision=HIGH
    ).reshape(tokens, state_rows)
    factor = float(lax.axis_size("dp") * lax.axis_size("ctx") * tokens) ** (-0.5)
    head_terms = jnp.stack([grads[5], grads[6], grads[7]]) * factor
    devices = lax.axis_size("dp") * lax.axis_size("ctx")
    spread = jnp.broadcast_to(head_terms[None], (devices,) + head_terms.shape)
    head_total = jnp.sum(lax.all_to_all(spread, ("dp", "ctx"), 0, 0, tiled=True), axis=0)
    features_gradient = grads[0].reshape(tokens, width).astype(jnp.bfloat16)[None]
    return (
        features_gradient,
        grads[1][None],
        (grads[2] + writer_extra)[None],
        (grads[3] + reader_extra)[None],
        head_total,
    )


def solution(mesh):
    placed = (
        P("dp", "ctx", None),
        P("dp", None, "ctx"),
        P("dp", "ctx", None),
        P("dp", "ctx", None),
        P(),
        P(),
        P(),
        P("dp", None),
        P("dp", "ctx", None),
    )
    return jax.shard_map(
        shards,
        mesh=mesh,
        in_specs=placed,
        out_specs=(
            P("dp", "ctx", None),
            P("dp", None, "ctx"),
            P("dp", "ctx", None),
            P("dp", "ctx", None),
            P(),
        ),
        check_vma=False,
    )
```

```python
import jax
import jax.numpy as jnp
from jax import lax
from jax.experimental import pallas as pl
from jax.sharding import PartitionSpec as P

GROUP = 128


HIGH = lax.Precision.HIGHEST


def scan_kernel(state_ref, pull_ref, decay_ref, out_ref):
    count = state_ref.shape[0]
    part = state_ref.shape[1]
    zero = jnp.zeros((part, out_ref.shape[2]), jnp.float32)

    def forward(j, state):
        out_ref[j, 0:part, :] = state
        return decay_ref[j] * state + state_ref[j]

    def backward(k, pull):
        j = count - 1 - k
        out_ref[j, part : 2 * part, :] = pull
        return decay_ref[j] * pull + pull_ref[j]

    lax.fori_loop(0, count, forward, zero)
    lax.fori_loop(0, count, backward, zero)


def exchange_scan(through, local_state, local_pull, axis):
    count = lax.axis_size(axis)
    rows, width = local_state.shape
    heads = through.shape[0]
    part = rows // count
    spare = 128 * ((heads + 127) // 128)
    extra = jnp.zeros((count, part, spare), jnp.float32).at[:, 0, :heads].set(through[None, :])
    sent_state = jnp.concatenate([local_state.reshape(count, part, width), extra], axis=2)
    moved_state = lax.all_to_all(sent_state, axis, 0, 0, tiled=True)
    moved_pull = lax.all_to_all(local_pull.reshape(count, part, width), axis, 0, 0, tiled=True)
    decays = jnp.repeat(moved_state[:, 0, width : width + heads], width // heads, axis=1)[:, None, :]
    lanes = 512 if width % 512 == 0 else width
    scanned = pl.pallas_call(
        scan_kernel,
        out_shape=jax.ShapeDtypeStruct((count, 2 * part, width), jnp.float32),
        grid=(width // lanes,),
        in_specs=[
            pl.BlockSpec((count, part, lanes), lambda c: (0, 0, c)),
            pl.BlockSpec((count, part, lanes), lambda c: (0, 0, c)),
            pl.BlockSpec((count, 1, lanes), lambda c: (0, 0, c)),
        ],
        out_specs=pl.BlockSpec((count, 2 * part, lanes), lambda c: (0, 0, c)),
    )(moved_state, moved_pull, decays)
    back = lax.all_to_all(scanned, axis, 0, 0, tiled=True)
    start_state = back[:, 0:part, :].reshape(rows, width)
    end_pull = back[:, part : 2 * part, :].reshape(rows, width)
    return start_state, end_pull


def group_step(
    state,
    prior_segment,
    inputs,
    log_decay,
    step_size,
    scores,
    reader_piece,
    writer_piece,
    segment_piece,
    skip_gain,
):
    size = inputs.shape[0]
    cumulative = jnp.cumsum(log_decay, axis=1)
    causal = jnp.arange(size)[:, None] >= jnp.arange(size)[None, :]
    within = causal & (segment_piece[:, None] == segment_piece[None, :])
    spread = cumulative[:, :, None] - cumulative[:, None, :]
    decay = jnp.where(within[None], jnp.exp(jnp.where(within[None], spread, 0.0)), 0.0)
    weights = decay * scores[None] * step_size[:, None, :]
    inner = jnp.einsum("hts,shp->thp", weights, inputs, precision=HIGH)
    carry_in = jnp.where((segment_piece == prior_segment)[None], jnp.exp(cumulative), 0.0)
    from_state = (
        jnp.einsum("tn,nhp->thp", reader_piece, state, precision=HIGH) * carry_in.T[:, :, None]
    )
    result = inner + from_state + skip_gain[None, :, None] * inputs
    to_end = (
        jnp.where(
            (segment_piece == segment_piece[-1])[None],
            jnp.exp(cumulative[:, -1:] - cumulative),
            0.0,
        )
        * step_size
    )
    fresh = jnp.einsum("hs,sn,shp->nhp", to_end, writer_piece, inputs, precision=HIGH)
    new_state = carry_in[:, -1][None, :, None] * state + fresh
    return (result, new_state)


def shards(
    features,
    step_logits,
    writer,
    reader,
    log_rates,
    step_bias,
    skip_gain,
    document_lengths,
    cotangent,
):
    tokens = features.shape[1]
    width = features.shape[2]
    heads = log_rates.shape[0]
    head_size = width // heads
    state_rows = writer.shape[2]
    blocks = tokens // GROUP
    position = lax.axis_index("ctx") * tokens + jnp.arange(tokens, dtype=jnp.int32)
    starts = jnp.cumsum(document_lengths[0])[:-1]
    segment = jnp.sum(position[:, None] >= starts[None, :], axis=1)
    prior_segment = jnp.sum(position[0] - 1 >= starts)
    inputs = features[0].astype(jnp.float32).reshape(tokens, heads, head_size)
    writer_full = writer[0].astype(jnp.float32)
    reader_full = reader[0].astype(jnp.float32)
    upstream = cotangent[0].astype(jnp.float32).reshape(tokens, heads, head_size)
    all_scores = jnp.einsum(
        "ctn,csn->cts",
        reader[0].reshape(blocks, GROUP, state_rows),
        writer[0].reshape(blocks, GROUP, state_rows),
        preferred_element_type=jnp.float32,
    )
    step_size = jax.nn.softplus(step_logits[0] + step_bias[:, None])
    log_decay = -jnp.exp(log_rates)[:, None] * step_size
    cumulative = jnp.cumsum(log_decay, axis=1)
    from_start = jnp.where((segment == prior_segment)[None], jnp.exp(cumulative), 0.0)
    through = from_start[:, -1]
    to_end = (
        jnp.where((segment == segment[-1])[None], jnp.exp(cumulative[:, -1:] - cumulative), 0.0)
        * step_size
    )
    local_state = jnp.einsum("hs,sn,shp->nhp", to_end, writer_full, inputs, precision=HIGH).reshape(
        state_rows, width
    )
    local_pull = jnp.einsum(
        "ht,tn,thp->nhp", from_start, reader_full, upstream, precision=HIGH
    ).reshape(state_rows, width)
    start_state, end_pull = exchange_scan(through, local_state, local_pull, "ctx")
    stepper = group_step

    def forward(inputs_in, logits, writer_in, reader_in, scores_in, rates, bias, gain):
        sizes_in = jax.nn.softplus(logits + bias[:, None])
        decays_in = -jnp.exp(rates)[:, None] * sizes_in
        state = start_state.reshape(state_rows, heads, head_size)
        prior = prior_segment
        results = []
        for number in range(blocks):
            first = number * GROUP
            final = first + GROUP
            result, state = stepper(
                state,
                prior,
                inputs_in[first:final],
                decays_in[:, first:final],
                sizes_in[:, first:final],
                scores_in[number],
                reader_in[first:final],
                writer_in[first:final],
                segment[first:final],
                gain,
            )
            prior = segment[final - 1]
            results.append(result)
        return (jnp.concatenate(results, axis=0), state)

    _, pullback = jax.vjp(
        forward,
        inputs,
        step_logits[0],
        writer_full,
        reader_full,
        all_scores,
        log_rates,
        step_bias,
        skip_gain,
    )
    grads = pullback((upstream, end_pull.reshape(state_rows, heads, head_size)))
    score_grads = grads[4]
    reader_extra = jnp.einsum(
        "cts,csn->ctn", score_grads, writer_full.reshape(blocks, GROUP, state_rows), precision=HIGH
    ).reshape(tokens, state_rows)
    writer_extra = jnp.einsum(
        "cts,ctn->csn", score_grads, reader_full.reshape(blocks, GROUP, state_rows), precision=HIGH
    ).reshape(tokens, state_rows)
    factor = float(lax.axis_size("dp") * lax.axis_size("ctx") * tokens) ** (-0.5)
    head_terms = jnp.stack([grads[5], grads[6], grads[7]]) * factor
    devices = lax.axis_size("dp") * lax.axis_size("ctx")
    spread = jnp.broadcast_to(head_terms[None], (devices,) + head_terms.shape)
    head_total = jnp.sum(lax.all_to_all(spread, ("dp", "ctx"), 0, 0, tiled=True), axis=0)
    features_gradient = grads[0].reshape(tokens, width).astype(jnp.bfloat16)[None]
    return (
        features_gradient,
        grads[1][None],
        (grads[2] + writer_extra)[None],
        (grads[3] + reader_extra)[None],
        head_total,
    )


def solution(mesh):
    placed = (
        P("dp", "ctx", None),
        P("dp", None, "ctx"),
        P("dp", "ctx", None),
        P("dp", "ctx", None),
        P(),
        P(),
        P(),
        P("dp", None),
        P("dp", "ctx", None),
    )
    return jax.shard_map(
        shards,
        mesh=mesh,
        in_specs=placed,
        out_specs=(
            P("dp", "ctx", None),
            P("dp", None, "ctx"),
            P("dp", "ctx", None),
            P("dp", "ctx", None),
            P(),
        ),
        check_vma=False,
    )
```

```python
import jax
import jax.numpy as jnp
from jax import lax
from jax.experimental import pallas as pl
from jax.sharding import PartitionSpec as P

GROUP = 128


HIGH = lax.Precision.HIGHEST


def scan_kernel(state_ref, pull_ref, decay_ref, out_ref):
    count = state_ref.shape[0]
    part = state_ref.shape[1]
    zero = jnp.zeros((part, out_ref.shape[2]), jnp.float32)

    def forward(j, state):
        out_ref[j, 0:part, :] = state
        return decay_ref[j] * state + state_ref[j]

    def backward(k, pull):
        j = count - 1 - k
        out_ref[j, part : 2 * part, :] = pull
        return decay_ref[j] * pull + pull_ref[j]

    lax.fori_loop(0, count, forward, zero)
    lax.fori_loop(0, count, backward, zero)


def exchange_scan(through, local_state, local_pull, axis):
    count = lax.axis_size(axis)
    rows, width = local_state.shape
    heads = through.shape[0]
    part = rows // count
    spare = 128 * ((heads + 127) // 128)
    extra = jnp.zeros((count, part, spare), jnp.float32).at[:, 0, :heads].set(through[None, :])
    sent_state = jnp.concatenate([local_state.reshape(count, part, width), extra], axis=2)
    moved_state = lax.all_to_all(sent_state, axis, 0, 0, tiled=True)
    moved_pull = lax.all_to_all(local_pull.reshape(count, part, width), axis, 0, 0, tiled=True)
    decays = jnp.repeat(moved_state[:, 0, width : width + heads], width // heads, axis=1)[:, None, :]
    lanes = 512 if width % 512 == 0 else width
    scanned = pl.pallas_call(
        scan_kernel,
        out_shape=jax.ShapeDtypeStruct((count, 2 * part, width), jnp.float32),
        grid=(width // lanes,),
        in_specs=[
            pl.BlockSpec((count, part, lanes), lambda c: (0, 0, c)),
            pl.BlockSpec((count, part, lanes), lambda c: (0, 0, c)),
            pl.BlockSpec((count, 1, lanes), lambda c: (0, 0, c)),
        ],
        out_specs=pl.BlockSpec((count, 2 * part, lanes), lambda c: (0, 0, c)),
    )(moved_state, moved_pull, decays)
    back = lax.all_to_all(scanned, axis, 0, 0, tiled=True)
    start_state = back[:, 0:part, :].reshape(rows, width)
    end_pull = back[:, part : 2 * part, :].reshape(rows, width)
    return start_state, end_pull


def group_step(
    state,
    prior_segment,
    inputs,
    log_decay,
    step_size,
    scores,
    reader_piece,
    writer_piece,
    segment_piece,
    skip_gain,
):
    size = inputs.shape[0]
    cumulative = jnp.cumsum(log_decay, axis=1)
    causal = jnp.arange(size)[:, None] >= jnp.arange(size)[None, :]
    within = causal & (segment_piece[:, None] == segment_piece[None, :])
    spread = cumulative[:, :, None] - cumulative[:, None, :]
    decay = jnp.where(within[None], jnp.exp(jnp.where(within[None], spread, 0.0)), 0.0)
    weights = decay * scores[None] * step_size[:, None, :]
    inner = jnp.einsum("hts,shp->thp", weights, inputs, precision=HIGH)
    carry_in = jnp.where((segment_piece == prior_segment)[None], jnp.exp(cumulative), 0.0)
    from_state = (
        jnp.einsum("tn,nhp->thp", reader_piece, state, precision=HIGH) * carry_in.T[:, :, None]
    )
    result = inner + from_state + skip_gain[None, :, None] * inputs
    to_end = (
        jnp.where(
            (segment_piece == segment_piece[-1])[None],
            jnp.exp(cumulative[:, -1:] - cumulative),
            0.0,
        )
        * step_size
    )
    fresh = jnp.einsum("hs,sn,shp->nhp", to_end, writer_piece, inputs, precision=HIGH)
    new_state = carry_in[:, -1][None, :, None] * state + fresh
    return (result, new_state)


def shards(
    features,
    step_logits,
    writer,
    reader,
    log_rates,
    step_bias,
    skip_gain,
    document_lengths,
    cotangent,
):
    tokens = features.shape[1]
    width = features.shape[2]
    heads = log_rates.shape[0]
    head_size = width // heads
    state_rows = writer.shape[2]
    blocks = tokens // GROUP
    position = lax.axis_index("ctx") * tokens + jnp.arange(tokens, dtype=jnp.int32)
    starts = jnp.cumsum(document_lengths[0])[:-1]
    segment = jnp.sum(position[:, None] >= starts[None, :], axis=1)
    prior_segment = jnp.sum(position[0] - 1 >= starts)
    inputs = features[0].astype(jnp.float32).reshape(tokens, heads, head_size)
    writer_full = writer[0].astype(jnp.float32)
    reader_full = reader[0].astype(jnp.float32)
    upstream = cotangent[0].astype(jnp.float32).reshape(tokens, heads, head_size)
    all_scores = jnp.einsum(
        "ctn,csn->cts",
        reader[0].reshape(blocks, GROUP, state_rows),
        writer[0].reshape(blocks, GROUP, state_rows),
        preferred_element_type=jnp.float32,
    )
    step_size = jax.nn.softplus(step_logits[0] + step_bias[:, None])
    log_decay = -jnp.exp(log_rates)[:, None] * step_size
    cumulative = jnp.cumsum(log_decay, axis=1)
    from_start = jnp.where((segment == prior_segment)[None], jnp.exp(cumulative), 0.0)
    through = from_start[:, -1]
    to_end = (
        jnp.where((segment == segment[-1])[None], jnp.exp(cumulative[:, -1:] - cumulative), 0.0)
        * step_size
    )
    local_state = jnp.dot(
        writer_full.T, (to_end.T[:, :, None] * inputs).reshape(tokens, width), precision=HIGH
    )
    local_pull = jnp.dot(
        reader_full.T, (from_start.T[:, :, None] * upstream).reshape(tokens, width), precision=HIGH
    )
    start_state, end_pull = exchange_scan(through, local_state, local_pull, "ctx")
    stepper = group_step

    def forward(inputs_in, logits, writer_in, reader_in, scores_in, rates, bias, gain):
        sizes_in = jax.nn.softplus(logits + bias[:, None])
        decays_in = -jnp.exp(rates)[:, None] * sizes_in
        state = start_state.reshape(state_rows, heads, head_size)
        prior = prior_segment
        results = []
        for number in range(blocks):
            first = number * GROUP
            final = first + GROUP
            result, state = stepper(
                state,
                prior,
                inputs_in[first:final],
                decays_in[:, first:final],
                sizes_in[:, first:final],
                scores_in[number],
                reader_in[first:final],
                writer_in[first:final],
                segment[first:final],
                gain,
            )
            prior = segment[final - 1]
            results.append(result)
        return (jnp.concatenate(results, axis=0), state)

    _, pullback = jax.vjp(
        forward,
        inputs,
        step_logits[0],
        writer_full,
        reader_full,
        all_scores,
        log_rates,
        step_bias,
        skip_gain,
    )
    grads = pullback((upstream, end_pull.reshape(state_rows, heads, head_size)))
    score_grads = grads[4]
    reader_extra = jnp.einsum(
        "cts,csn->ctn", score_grads, writer_full.reshape(blocks, GROUP, state_rows), precision=HIGH
    ).reshape(tokens, state_rows)
    writer_extra = jnp.einsum(
        "cts,ctn->csn", score_grads, reader_full.reshape(blocks, GROUP, state_rows), precision=HIGH
    ).reshape(tokens, state_rows)
    factor = float(lax.axis_size("dp") * lax.axis_size("ctx") * tokens) ** (-0.5)
    head_terms = jnp.stack([grads[5], grads[6], grads[7]]) * factor
    devices = lax.axis_size("dp") * lax.axis_size("ctx")
    spread = jnp.broadcast_to(head_terms[None], (devices,) + head_terms.shape)
    head_total = jnp.sum(lax.all_to_all(spread, ("dp", "ctx"), 0, 0, tiled=True), axis=0)
    features_gradient = grads[0].reshape(tokens, width).astype(jnp.bfloat16)[None]
    return (
        features_gradient,
        grads[1][None],
        (grads[2] + writer_extra)[None],
        (grads[3] + reader_extra)[None],
        head_total,
    )


def solution(mesh):
    placed = (
        P("dp", "ctx", None),
        P("dp", None, "ctx"),
        P("dp", "ctx", None),
        P("dp", "ctx", None),
        P(),
        P(),
        P(),
        P("dp", None),
        P("dp", "ctx", None),
    )
    return jax.shard_map(
        shards,
        mesh=mesh,
        in_specs=placed,
        out_specs=(
            P("dp", "ctx", None),
            P("dp", None, "ctx"),
            P("dp", "ctx", None),
            P("dp", "ctx", None),
            P(),
        ),
        check_vma=False,
    )
```

```python
import jax
import jax.numpy as jnp
from jax import lax
from jax.experimental import pallas as pl
from jax.sharding import PartitionSpec as P

GROUP = 128


HIGH = lax.Precision.HIGHEST


def forward_kernel(moved_ref, decay_ref, out_ref):
    def step(j, state):
        out_ref[j] = state
        return decay_ref[j] * state + moved_ref[j]

    lax.fori_loop(0, moved_ref.shape[0], step, jnp.zeros(out_ref.shape[1:], jnp.float32))


def backward_kernel(moved_ref, decay_ref, out_ref):
    count = moved_ref.shape[0]

    def step(k, pull):
        j = count - 1 - k
        out_ref[j] = pull
        return decay_ref[j] * pull + moved_ref[j]

    lax.fori_loop(0, count, step, jnp.zeros(out_ref.shape[1:], jnp.float32))


def gather_ring(value, axis):
    count = lax.axis_size(axis)
    mine = lax.axis_index(axis)
    held = value[None]
    shift = 1
    while shift < count:
        pairs = [(i, (i + shift) % count) for i in range(count)]
        held = jnp.concatenate([held, lax.ppermute(held, axis, pairs)], axis=0)
        shift *= 2
    return held[(mine - jnp.arange(count)) % count]


def exchange_scan(through, local_state, local_pull, axis):
    count = lax.axis_size(axis)
    rows, width = local_state.shape
    heads = through.shape[0]
    half = count // 2
    part = rows // half
    decays = jnp.repeat(gather_ring(through, axis), width // heads, axis=1)[:, None, :]
    sent = jnp.concatenate(
        [local_state.reshape(half, part, width), local_pull.reshape(half, part, width)], axis=0
    )
    moved = lax.all_to_all(sent, axis, 0, 0, tiled=True)
    lanes = 512 if width % 512 == 0 else width

    def scan_with(kernel):
        return pl.pallas_call(
            kernel,
            out_shape=jax.ShapeDtypeStruct((count, part, width), jnp.float32),
            grid=(width // lanes,),
            in_specs=[
                pl.BlockSpec((count, part, lanes), lambda c: (0, 0, c)),
                pl.BlockSpec((count, 1, lanes), lambda c: (0, 0, c)),
            ],
            out_specs=pl.BlockSpec((count, part, lanes), lambda c: (0, 0, c)),
        )

    scanned = lax.cond(
        lax.axis_index(axis) < half,
        scan_with(forward_kernel),
        scan_with(backward_kernel),
        moved,
        decays,
    )
    back = lax.all_to_all(scanned, axis, 0, 0, tiled=True)
    return back[:half].reshape(rows, width), back[half:].reshape(rows, width)


def group_step(
    state,
    prior_segment,
    inputs,
    log_decay,
    step_size,
    scores,
    reader_piece,
    writer_piece,
    segment_piece,
    skip_gain,
):
    size = inputs.shape[0]
    cumulative = jnp.cumsum(log_decay, axis=1)
    causal = jnp.arange(size)[:, None] >= jnp.arange(size)[None, :]
    within = causal & (segment_piece[:, None] == segment_piece[None, :])
    spread = cumulative[:, :, None] - cumulative[:, None, :]
    decay = jnp.where(within[None], jnp.exp(jnp.where(within[None], spread, 0.0)), 0.0)
    weights = decay * scores[None] * step_size[:, None, :]
    inner = jnp.einsum("hts,shp->thp", weights, inputs, precision=HIGH)
    carry_in = jnp.where((segment_piece == prior_segment)[None], jnp.exp(cumulative), 0.0)
    from_state = (
        jnp.einsum("tn,nhp->thp", reader_piece, state, precision=HIGH) * carry_in.T[:, :, None]
    )
    result = inner + from_state + skip_gain[None, :, None] * inputs
    to_end = (
        jnp.where(
            (segment_piece == segment_piece[-1])[None],
            jnp.exp(cumulative[:, -1:] - cumulative),
            0.0,
        )
        * step_size
    )
    fresh = jnp.einsum("hs,sn,shp->nhp", to_end, writer_piece, inputs, precision=HIGH)
    new_state = carry_in[:, -1][None, :, None] * state + fresh
    return (result, new_state)


def shards(
    features,
    step_logits,
    writer,
    reader,
    log_rates,
    step_bias,
    skip_gain,
    document_lengths,
    cotangent,
):
    tokens = features.shape[1]
    width = features.shape[2]
    heads = log_rates.shape[0]
    head_size = width // heads
    state_rows = writer.shape[2]
    blocks = tokens // GROUP
    position = lax.axis_index("ctx") * tokens + jnp.arange(tokens, dtype=jnp.int32)
    starts = jnp.cumsum(document_lengths[0])[:-1]
    segment = jnp.sum(position[:, None] >= starts[None, :], axis=1)
    prior_segment = jnp.sum(position[0] - 1 >= starts)
    inputs = features[0].astype(jnp.float32).reshape(tokens, heads, head_size)
    writer_full = writer[0].astype(jnp.float32)
    reader_full = reader[0].astype(jnp.float32)
    upstream = cotangent[0].astype(jnp.float32).reshape(tokens, heads, head_size)
    all_scores = jnp.einsum(
        "ctn,csn->cts",
        reader[0].reshape(blocks, GROUP, state_rows),
        writer[0].reshape(blocks, GROUP, state_rows),
        preferred_element_type=jnp.float32,
    )
    step_size = jax.nn.softplus(step_logits[0] + step_bias[:, None])
    log_decay = -jnp.exp(log_rates)[:, None] * step_size
    cumulative = jnp.cumsum(log_decay, axis=1)
    from_start = jnp.where((segment == prior_segment)[None], jnp.exp(cumulative), 0.0)
    through = from_start[:, -1]
    to_end = (
        jnp.where((segment == segment[-1])[None], jnp.exp(cumulative[:, -1:] - cumulative), 0.0)
        * step_size
    )
    local_state = jnp.dot(
        writer_full.T, (to_end.T[:, :, None] * inputs).reshape(tokens, width), precision=HIGH
    )
    local_pull = jnp.dot(
        reader_full.T, (from_start.T[:, :, None] * upstream).reshape(tokens, width), precision=HIGH
    )
    start_state, end_pull = exchange_scan(through, local_state, local_pull, "ctx")
    stepper = group_step

    def forward(inputs_in, logits, writer_in, reader_in, scores_in, rates, bias, gain):
        sizes_in = jax.nn.softplus(logits + bias[:, None])
        decays_in = -jnp.exp(rates)[:, None] * sizes_in
        state = start_state.reshape(state_rows, heads, head_size)
        prior = prior_segment
        results = []
        for number in range(blocks):
            first = number * GROUP
            final = first + GROUP
            result, state = stepper(
                state,
                prior,
                inputs_in[first:final],
                decays_in[:, first:final],
                sizes_in[:, first:final],
                scores_in[number],
                reader_in[first:final],
                writer_in[first:final],
                segment[first:final],
                gain,
            )
            prior = segment[final - 1]
            results.append(result)
        return (jnp.concatenate(results, axis=0), state)

    _, pullback = jax.vjp(
        forward,
        inputs,
        step_logits[0],
        writer_full,
        reader_full,
        all_scores,
        log_rates,
        step_bias,
        skip_gain,
    )
    grads = pullback((upstream, end_pull.reshape(state_rows, heads, head_size)))
    score_grads = grads[4]
    reader_extra = jnp.einsum(
        "cts,csn->ctn", score_grads, writer_full.reshape(blocks, GROUP, state_rows), precision=HIGH
    ).reshape(tokens, state_rows)
    writer_extra = jnp.einsum(
        "cts,ctn->csn", score_grads, reader_full.reshape(blocks, GROUP, state_rows), precision=HIGH
    ).reshape(tokens, state_rows)
    factor = float(lax.axis_size("dp") * lax.axis_size("ctx") * tokens) ** (-0.5)
    head_terms = jnp.stack([grads[5], grads[6], grads[7]]) * factor
    devices = lax.axis_size("dp") * lax.axis_size("ctx")
    spread = jnp.broadcast_to(head_terms[None], (devices,) + head_terms.shape)
    head_total = jnp.sum(lax.all_to_all(spread, ("dp", "ctx"), 0, 0, tiled=True), axis=0)
    features_gradient = grads[0].reshape(tokens, width).astype(jnp.bfloat16)[None]
    return (
        features_gradient,
        grads[1][None],
        (grads[2] + writer_extra)[None],
        (grads[3] + reader_extra)[None],
        head_total,
    )


def solution(mesh):
    placed = (
        P("dp", "ctx", None),
        P("dp", None, "ctx"),
        P("dp", "ctx", None),
        P("dp", "ctx", None),
        P(),
        P(),
        P(),
        P("dp", None),
        P("dp", "ctx", None),
    )
    return jax.shard_map(
        shards,
        mesh=mesh,
        in_specs=placed,
        out_specs=(
            P("dp", "ctx", None),
            P("dp", None, "ctx"),
            P("dp", "ctx", None),
            P("dp", "ctx", None),
            P(),
        ),
        check_vma=False,
    )
```

```python
import jax
import jax.numpy as jnp
from jax import lax
from jax.experimental import pallas as pl
from jax.sharding import PartitionSpec as P

GROUP = 128


HIGH = lax.Precision.HIGHEST


def forward_kernel(moved_ref, decay_ref, out_ref):
    def step(j, state):
        out_ref[j] = state
        return decay_ref[j] * state + moved_ref[j]

    lax.fori_loop(0, moved_ref.shape[0], step, jnp.zeros(out_ref.shape[1:], jnp.float32))


def backward_kernel(moved_ref, decay_ref, out_ref):
    count = moved_ref.shape[0]

    def step(k, pull):
        j = count - 1 - k
        out_ref[j] = pull
        return decay_ref[j] * pull + moved_ref[j]

    lax.fori_loop(0, count, step, jnp.zeros(out_ref.shape[1:], jnp.float32))


def gather_ring(value, axis):
    count = lax.axis_size(axis)
    mine = lax.axis_index(axis)
    held = value[None]
    shift = 1
    while shift < count:
        pairs = [(i, (i + shift) % count) for i in range(count)]
        held = jnp.concatenate([held, lax.ppermute(held, axis, pairs)], axis=0)
        shift *= 2
    return held[(mine - jnp.arange(count)) % count]


def exchange_scan(through, local_state, local_pull, axis):
    count = lax.axis_size(axis)
    rows, width = local_state.shape
    heads = through.shape[0]
    half = count // 2
    part = rows // half
    decays = jnp.repeat(gather_ring(through, axis), width // heads, axis=1)[:, None, :]
    sent = jnp.concatenate(
        [local_state.reshape(half, part, width), local_pull.reshape(half, part, width)], axis=0
    )
    sent, decays = lax.optimization_barrier((sent, decays))
    moved = lax.all_to_all(sent, axis, 0, 0, tiled=True)
    lanes = 512 if width % 512 == 0 else width

    def scan_with(kernel):
        return pl.pallas_call(
            kernel,
            out_shape=jax.ShapeDtypeStruct((count, part, width), jnp.float32),
            grid=(width // lanes,),
            in_specs=[
                pl.BlockSpec((count, part, lanes), lambda c: (0, 0, c)),
                pl.BlockSpec((count, 1, lanes), lambda c: (0, 0, c)),
            ],
            out_specs=pl.BlockSpec((count, part, lanes), lambda c: (0, 0, c)),
        )

    scanned = lax.cond(
        lax.axis_index(axis) < half,
        scan_with(forward_kernel),
        scan_with(backward_kernel),
        moved,
        decays,
    )
    back = lax.all_to_all(scanned, axis, 0, 0, tiled=True)
    return back[:half].reshape(rows, width), back[half:].reshape(rows, width)


def group_step(
    state,
    prior_segment,
    inputs,
    log_decay,
    step_size,
    scores,
    reader_piece,
    writer_piece,
    segment_piece,
    skip_gain,
):
    size = inputs.shape[0]
    cumulative = jnp.cumsum(log_decay, axis=1)
    causal = jnp.arange(size)[:, None] >= jnp.arange(size)[None, :]
    within = causal & (segment_piece[:, None] == segment_piece[None, :])
    spread = cumulative[:, :, None] - cumulative[:, None, :]
    decay = jnp.where(within[None], jnp.exp(jnp.where(within[None], spread, 0.0)), 0.0)
    weights = decay * scores[None] * step_size[:, None, :]
    inner = jnp.einsum("hts,shp->thp", weights, inputs, precision=HIGH)
    carry_in = jnp.where((segment_piece == prior_segment)[None], jnp.exp(cumulative), 0.0)
    from_state = (
        jnp.einsum("tn,nhp->thp", reader_piece, state, precision=HIGH) * carry_in.T[:, :, None]
    )
    result = inner + from_state + skip_gain[None, :, None] * inputs
    to_end = (
        jnp.where(
            (segment_piece == segment_piece[-1])[None],
            jnp.exp(cumulative[:, -1:] - cumulative),
            0.0,
        )
        * step_size
    )
    fresh = jnp.einsum("hs,sn,shp->nhp", to_end, writer_piece, inputs, precision=HIGH)
    new_state = carry_in[:, -1][None, :, None] * state + fresh
    return (result, new_state)


def shards(
    features,
    step_logits,
    writer,
    reader,
    log_rates,
    step_bias,
    skip_gain,
    document_lengths,
    cotangent,
):
    tokens = features.shape[1]
    width = features.shape[2]
    heads = log_rates.shape[0]
    head_size = width // heads
    state_rows = writer.shape[2]
    blocks = tokens // GROUP
    position = lax.axis_index("ctx") * tokens + jnp.arange(tokens, dtype=jnp.int32)
    starts = jnp.cumsum(document_lengths[0])[:-1]
    segment = jnp.sum(position[:, None] >= starts[None, :], axis=1)
    prior_segment = jnp.sum(position[0] - 1 >= starts)
    inputs = features[0].astype(jnp.float32).reshape(tokens, heads, head_size)
    writer_full = writer[0].astype(jnp.float32)
    reader_full = reader[0].astype(jnp.float32)
    upstream = cotangent[0].astype(jnp.float32).reshape(tokens, heads, head_size)
    all_scores = jnp.einsum(
        "ctn,csn->cts",
        reader[0].reshape(blocks, GROUP, state_rows),
        writer[0].reshape(blocks, GROUP, state_rows),
        preferred_element_type=jnp.float32,
    )
    step_size = jax.nn.softplus(step_logits[0] + step_bias[:, None])
    log_decay = -jnp.exp(log_rates)[:, None] * step_size
    cumulative = jnp.cumsum(log_decay, axis=1)
    from_start = jnp.where((segment == prior_segment)[None], jnp.exp(cumulative), 0.0)
    through = from_start[:, -1]
    to_end = (
        jnp.where((segment == segment[-1])[None], jnp.exp(cumulative[:, -1:] - cumulative), 0.0)
        * step_size
    )
    local_state = jnp.dot(
        writer_full.T, (to_end.T[:, :, None] * inputs).reshape(tokens, width), precision=HIGH
    )
    local_pull = jnp.dot(
        reader_full.T, (from_start.T[:, :, None] * upstream).reshape(tokens, width), precision=HIGH
    )
    start_state, end_pull = exchange_scan(through, local_state, local_pull, "ctx")
    stepper = group_step

    def forward(inputs_in, logits, writer_in, reader_in, scores_in, rates, bias, gain):
        sizes_in = jax.nn.softplus(logits + bias[:, None])
        decays_in = -jnp.exp(rates)[:, None] * sizes_in
        state = start_state.reshape(state_rows, heads, head_size)
        prior = prior_segment
        results = []
        for number in range(blocks):
            first = number * GROUP
            final = first + GROUP
            result, state = stepper(
                state,
                prior,
                inputs_in[first:final],
                decays_in[:, first:final],
                sizes_in[:, first:final],
                scores_in[number],
                reader_in[first:final],
                writer_in[first:final],
                segment[first:final],
                gain,
            )
            prior = segment[final - 1]
            results.append(result)
        return (jnp.concatenate(results, axis=0), state)

    _, pullback = jax.vjp(
        forward,
        inputs,
        step_logits[0],
        writer_full,
        reader_full,
        all_scores,
        log_rates,
        step_bias,
        skip_gain,
    )
    grads = pullback((upstream, end_pull.reshape(state_rows, heads, head_size)))
    score_grads = grads[4]
    reader_extra = jnp.einsum(
        "cts,csn->ctn", score_grads, writer_full.reshape(blocks, GROUP, state_rows), precision=HIGH
    ).reshape(tokens, state_rows)
    writer_extra = jnp.einsum(
        "cts,ctn->csn", score_grads, reader_full.reshape(blocks, GROUP, state_rows), precision=HIGH
    ).reshape(tokens, state_rows)
    factor = float(lax.axis_size("dp") * lax.axis_size("ctx") * tokens) ** (-0.5)
    head_terms = jnp.stack([grads[5], grads[6], grads[7]]) * factor
    devices = lax.axis_size("dp") * lax.axis_size("ctx")
    spread = jnp.broadcast_to(head_terms[None], (devices,) + head_terms.shape)
    head_total = jnp.sum(lax.all_to_all(spread, ("dp", "ctx"), 0, 0, tiled=True), axis=0)
    features_gradient = grads[0].reshape(tokens, width).astype(jnp.bfloat16)[None]
    return (
        features_gradient,
        grads[1][None],
        (grads[2] + writer_extra)[None],
        (grads[3] + reader_extra)[None],
        head_total,
    )


def solution(mesh):
    placed = (
        P("dp", "ctx", None),
        P("dp", None, "ctx"),
        P("dp", "ctx", None),
        P("dp", "ctx", None),
        P(),
        P(),
        P(),
        P("dp", None),
        P("dp", "ctx", None),
    )
    return jax.shard_map(
        shards,
        mesh=mesh,
        in_specs=placed,
        out_specs=(
            P("dp", "ctx", None),
            P("dp", None, "ctx"),
            P("dp", "ctx", None),
            P("dp", "ctx", None),
            P(),
        ),
        check_vma=False,
    )
```

```python
import jax
import jax.numpy as jnp
from jax import lax
from jax.experimental import pallas as pl
from jax.sharding import PartitionSpec as P

GROUP = 128


HIGH = lax.Precision.HIGHEST


def forward_kernel(moved_ref, decay_ref, out_ref):
    def step(j, state):
        out_ref[j] = state
        return decay_ref[j] * state + moved_ref[j]

    lax.fori_loop(0, moved_ref.shape[0], step, jnp.zeros(out_ref.shape[1:], jnp.float32))


def backward_kernel(moved_ref, decay_ref, out_ref):
    count = moved_ref.shape[0]

    def step(k, pull):
        j = count - 1 - k
        out_ref[j] = pull
        return decay_ref[j] * pull + moved_ref[j]

    lax.fori_loop(0, count, step, jnp.zeros(out_ref.shape[1:], jnp.float32))


def gather_ring(value, axis, radix=8):
    count = lax.axis_size(axis)
    mine = lax.axis_index(axis)
    held = value[None]
    have = 1
    while have < count:
        fan = min(radix, -(-count // have))
        pieces = [held]
        for m in range(1, fan):
            shift = have * m
            pairs = [(i, (i + shift) % count) for i in range(count)]
            pieces.append(lax.ppermute(held, axis, pairs))
        held = jnp.concatenate(pieces, axis=0)
        have *= fan
    return held[(mine - jnp.arange(count)) % count]


def exchange_scan(through, local_state, local_pull, axis):
    count = lax.axis_size(axis)
    rows, width = local_state.shape
    heads = through.shape[0]
    half = count // 2
    part = rows // half
    decays = jnp.repeat(gather_ring(through, axis), width // heads, axis=1)[:, None, :]
    sent = jnp.concatenate(
        [local_state.reshape(half, part, width), local_pull.reshape(half, part, width)], axis=0
    )
    sent, decays = lax.optimization_barrier((sent, decays))
    moved = lax.all_to_all(sent, axis, 0, 0, tiled=True)
    lanes = 512 if width % 512 == 0 else width

    def scan_with(kernel):
        return pl.pallas_call(
            kernel,
            out_shape=jax.ShapeDtypeStruct((count, part, width), jnp.float32),
            grid=(width // lanes,),
            in_specs=[
                pl.BlockSpec((count, part, lanes), lambda c: (0, 0, c)),
                pl.BlockSpec((count, 1, lanes), lambda c: (0, 0, c)),
            ],
            out_specs=pl.BlockSpec((count, part, lanes), lambda c: (0, 0, c)),
        )

    scanned = lax.cond(
        lax.axis_index(axis) < half,
        scan_with(forward_kernel),
        scan_with(backward_kernel),
        moved,
        decays,
    )
    back = lax.all_to_all(scanned, axis, 0, 0, tiled=True)
    return back[:half].reshape(rows, width), back[half:].reshape(rows, width)


def group_step(
    state,
    prior_segment,
    inputs,
    log_decay,
    step_size,
    scores,
    reader_piece,
    writer_piece,
    segment_piece,
    skip_gain,
):
    size = inputs.shape[0]
    cumulative = jnp.cumsum(log_decay, axis=1)
    causal = jnp.arange(size)[:, None] >= jnp.arange(size)[None, :]
    within = causal & (segment_piece[:, None] == segment_piece[None, :])
    spread = cumulative[:, :, None] - cumulative[:, None, :]
    decay = jnp.where(within[None], jnp.exp(jnp.where(within[None], spread, 0.0)), 0.0)
    weights = decay * scores[None] * step_size[:, None, :]
    inner = jnp.einsum("hts,shp->thp", weights, inputs, precision=HIGH)
    carry_in = jnp.where((segment_piece == prior_segment)[None], jnp.exp(cumulative), 0.0)
    from_state = (
        jnp.einsum("tn,nhp->thp", reader_piece, state, precision=HIGH) * carry_in.T[:, :, None]
    )
    result = inner + from_state + skip_gain[None, :, None] * inputs
    to_end = (
        jnp.where(
            (segment_piece == segment_piece[-1])[None],
            jnp.exp(cumulative[:, -1:] - cumulative),
            0.0,
        )
        * step_size
    )
    fresh = jnp.einsum("hs,sn,shp->nhp", to_end, writer_piece, inputs, precision=HIGH)
    new_state = carry_in[:, -1][None, :, None] * state + fresh
    return (result, new_state)


def shards(
    features,
    step_logits,
    writer,
    reader,
    log_rates,
    step_bias,
    skip_gain,
    document_lengths,
    cotangent,
):
    tokens = features.shape[1]
    width = features.shape[2]
    heads = log_rates.shape[0]
    head_size = width // heads
    state_rows = writer.shape[2]
    blocks = tokens // GROUP
    position = lax.axis_index("ctx") * tokens + jnp.arange(tokens, dtype=jnp.int32)
    starts = jnp.cumsum(document_lengths[0])[:-1]
    segment = jnp.sum(position[:, None] >= starts[None, :], axis=1)
    prior_segment = jnp.sum(position[0] - 1 >= starts)
    inputs = features[0].astype(jnp.float32).reshape(tokens, heads, head_size)
    writer_full = writer[0].astype(jnp.float32)
    reader_full = reader[0].astype(jnp.float32)
    upstream = cotangent[0].astype(jnp.float32).reshape(tokens, heads, head_size)
    all_scores = jnp.einsum(
        "ctn,csn->cts",
        reader[0].reshape(blocks, GROUP, state_rows),
        writer[0].reshape(blocks, GROUP, state_rows),
        preferred_element_type=jnp.float32,
    )
    step_size = jax.nn.softplus(step_logits[0] + step_bias[:, None])
    log_decay = -jnp.exp(log_rates)[:, None] * step_size
    cumulative = jnp.cumsum(log_decay, axis=1)
    from_start = jnp.where((segment == prior_segment)[None], jnp.exp(cumulative), 0.0)
    through = from_start[:, -1]
    to_end = (
        jnp.where((segment == segment[-1])[None], jnp.exp(cumulative[:, -1:] - cumulative), 0.0)
        * step_size
    )
    local_state = jnp.dot(
        writer_full.T, (to_end.T[:, :, None] * inputs).reshape(tokens, width), precision=HIGH
    )
    local_pull = jnp.dot(
        reader_full.T, (from_start.T[:, :, None] * upstream).reshape(tokens, width), precision=HIGH
    )
    start_state, end_pull = exchange_scan(through, local_state, local_pull, "ctx")
    stepper = group_step

    def forward(inputs_in, logits, writer_in, reader_in, scores_in, rates, bias, gain):
        sizes_in = jax.nn.softplus(logits + bias[:, None])
        decays_in = -jnp.exp(rates)[:, None] * sizes_in
        state = start_state.reshape(state_rows, heads, head_size)
        prior = prior_segment
        results = []
        for number in range(blocks):
            first = number * GROUP
            final = first + GROUP
            result, state = stepper(
                state,
                prior,
                inputs_in[first:final],
                decays_in[:, first:final],
                sizes_in[:, first:final],
                scores_in[number],
                reader_in[first:final],
                writer_in[first:final],
                segment[first:final],
                gain,
            )
            prior = segment[final - 1]
            results.append(result)
        return (jnp.concatenate(results, axis=0), state)

    _, pullback = jax.vjp(
        forward,
        inputs,
        step_logits[0],
        writer_full,
        reader_full,
        all_scores,
        log_rates,
        step_bias,
        skip_gain,
    )
    grads = pullback((upstream, end_pull.reshape(state_rows, heads, head_size)))
    score_grads = grads[4]
    reader_extra = jnp.einsum(
        "cts,csn->ctn", score_grads, writer_full.reshape(blocks, GROUP, state_rows), precision=HIGH
    ).reshape(tokens, state_rows)
    writer_extra = jnp.einsum(
        "cts,ctn->csn", score_grads, reader_full.reshape(blocks, GROUP, state_rows), precision=HIGH
    ).reshape(tokens, state_rows)
    factor = float(lax.axis_size("dp") * lax.axis_size("ctx") * tokens) ** (-0.5)
    head_terms = jnp.stack([grads[5], grads[6], grads[7]]) * factor
    devices = lax.axis_size("dp") * lax.axis_size("ctx")
    spread = jnp.broadcast_to(head_terms[None], (devices,) + head_terms.shape)
    head_total = jnp.sum(lax.all_to_all(spread, ("dp", "ctx"), 0, 0, tiled=True), axis=0)
    features_gradient = grads[0].reshape(tokens, width).astype(jnp.bfloat16)[None]
    return (
        features_gradient,
        grads[1][None],
        (grads[2] + writer_extra)[None],
        (grads[3] + reader_extra)[None],
        head_total,
    )


def solution(mesh):
    placed = (
        P("dp", "ctx", None),
        P("dp", None, "ctx"),
        P("dp", "ctx", None),
        P("dp", "ctx", None),
        P(),
        P(),
        P(),
        P("dp", None),
        P("dp", "ctx", None),
    )
    return jax.shard_map(
        shards,
        mesh=mesh,
        in_specs=placed,
        out_specs=(
            P("dp", "ctx", None),
            P("dp", None, "ctx"),
            P("dp", "ctx", None),
            P("dp", "ctx", None),
            P(),
        ),
        check_vma=False,
    )
```

```python
import jax
import jax.numpy as jnp
from jax import lax
from jax.experimental import pallas as pl
from jax.sharding import PartitionSpec as P

GROUP = 128


HIGH = lax.Precision.HIGHEST


def forward_kernel(moved_ref, decay_ref, out_ref):
    def step(j, state):
        out_ref[j] = state
        return decay_ref[j] * state + moved_ref[j]

    lax.fori_loop(0, moved_ref.shape[0], step, jnp.zeros(out_ref.shape[1:], jnp.float32))


def backward_kernel(moved_ref, decay_ref, out_ref):
    count = moved_ref.shape[0]

    def step(k, pull):
        j = count - 1 - k
        out_ref[j] = pull
        return decay_ref[j] * pull + moved_ref[j]

    lax.fori_loop(0, count, step, jnp.zeros(out_ref.shape[1:], jnp.float32))


def exchange_scan(through, local_state, local_pull, axis):
    count = lax.axis_size(axis)
    rows, width = local_state.shape
    heads = through.shape[0]
    half = count // 2
    part = rows // half
    sent = jnp.concatenate(
        [
            local_state.reshape(half, part, width),
            local_pull.reshape(half, part, width),
        ],
        axis=0,
    )
    spare = 128 * ((heads + 127) // 128)
    extra = jnp.zeros((count, part, spare), jnp.float32).at[:, 0, :heads].set(through[None, :])
    moved = lax.all_to_all(jnp.concatenate([sent, extra], axis=2), axis, 0, 0, tiled=True)
    decays = jnp.repeat(moved[:, 0, width : width + heads], width // heads, axis=1)[:, None, :]
    lanes = 512 if width % 512 == 0 else width

    def scan_with(kernel):
        return pl.pallas_call(
            kernel,
            out_shape=jax.ShapeDtypeStruct((count, part, width), jnp.float32),
            grid=(width // lanes,),
            in_specs=[
                pl.BlockSpec((count, part, lanes), lambda c: (0, 0, c)),
                pl.BlockSpec((count, 1, lanes), lambda c: (0, 0, c)),
            ],
            out_specs=pl.BlockSpec((count, part, lanes), lambda c: (0, 0, c)),
        )

    scanned = lax.cond(
        lax.axis_index(axis) < half,
        scan_with(forward_kernel),
        scan_with(backward_kernel),
        moved,
        decays,
    )
    back = lax.all_to_all(scanned, axis, 0, 0, tiled=True)
    return back[:half].reshape(rows, width), back[half:].reshape(rows, width)


def group_step(
    state,
    prior_segment,
    inputs,
    log_decay,
    step_size,
    scores,
    reader_piece,
    writer_piece,
    segment_piece,
    skip_gain,
):
    size = inputs.shape[0]
    cumulative = jnp.cumsum(log_decay, axis=1)
    causal = jnp.arange(size)[:, None] >= jnp.arange(size)[None, :]
    within = causal & (segment_piece[:, None] == segment_piece[None, :])
    spread = cumulative[:, :, None] - cumulative[:, None, :]
    decay = jnp.where(within[None], jnp.exp(jnp.where(within[None], spread, 0.0)), 0.0)
    weights = decay * scores[None] * step_size[:, None, :]
    inner = jnp.einsum("hts,shp->thp", weights, inputs, precision=HIGH)
    carry_in = jnp.where((segment_piece == prior_segment)[None], jnp.exp(cumulative), 0.0)
    from_state = (
        jnp.einsum("tn,nhp->thp", reader_piece, state, precision=HIGH) * carry_in.T[:, :, None]
    )
    result = inner + from_state + skip_gain[None, :, None] * inputs
    to_end = (
        jnp.where(
            (segment_piece == segment_piece[-1])[None],
            jnp.exp(cumulative[:, -1:] - cumulative),
            0.0,
        )
        * step_size
    )
    fresh = jnp.einsum("hs,sn,shp->nhp", to_end, writer_piece, inputs, precision=HIGH)
    new_state = carry_in[:, -1][None, :, None] * state + fresh
    return (result, new_state)


def shards(
    features,
    step_logits,
    writer,
    reader,
    log_rates,
    step_bias,
    skip_gain,
    document_lengths,
    cotangent,
):
    tokens = features.shape[1]
    width = features.shape[2]
    heads = log_rates.shape[0]
    head_size = width // heads
    state_rows = writer.shape[2]
    blocks = tokens // GROUP
    position = lax.axis_index("ctx") * tokens + jnp.arange(tokens, dtype=jnp.int32)
    starts = jnp.cumsum(document_lengths[0])[:-1]
    segment = jnp.sum(position[:, None] >= starts[None, :], axis=1)
    prior_segment = jnp.sum(position[0] - 1 >= starts)
    inputs = features[0].astype(jnp.float32).reshape(tokens, heads, head_size)
    writer_full = writer[0].astype(jnp.float32)
    reader_full = reader[0].astype(jnp.float32)
    upstream = cotangent[0].astype(jnp.float32).reshape(tokens, heads, head_size)
    all_scores = jnp.einsum(
        "ctn,csn->cts",
        reader[0].reshape(blocks, GROUP, state_rows),
        writer[0].reshape(blocks, GROUP, state_rows),
        preferred_element_type=jnp.float32,
    )
    step_size = jax.nn.softplus(step_logits[0] + step_bias[:, None])
    log_decay = -jnp.exp(log_rates)[:, None] * step_size
    cumulative = jnp.cumsum(log_decay, axis=1)
    from_start = jnp.where((segment == prior_segment)[None], jnp.exp(cumulative), 0.0)
    through = from_start[:, -1]
    to_end = (
        jnp.where((segment == segment[-1])[None], jnp.exp(cumulative[:, -1:] - cumulative), 0.0)
        * step_size
    )
    local_state = jnp.dot(
        writer_full.T, (to_end.T[:, :, None] * inputs).reshape(tokens, width), precision=HIGH
    )
    local_pull = jnp.dot(
        reader_full.T, (from_start.T[:, :, None] * upstream).reshape(tokens, width), precision=HIGH
    )
    start_state, end_pull = exchange_scan(through, local_state, local_pull, "ctx")
    stepper = group_step

    def forward(inputs_in, logits, writer_in, reader_in, scores_in, rates, bias, gain):
        sizes_in = jax.nn.softplus(logits + bias[:, None])
        decays_in = -jnp.exp(rates)[:, None] * sizes_in
        state = start_state.reshape(state_rows, heads, head_size)
        prior = prior_segment
        results = []
        for number in range(blocks):
            first = number * GROUP
            final = first + GROUP
            result, state = stepper(
                state,
                prior,
                inputs_in[first:final],
                decays_in[:, first:final],
                sizes_in[:, first:final],
                scores_in[number],
                reader_in[first:final],
                writer_in[first:final],
                segment[first:final],
                gain,
            )
            prior = segment[final - 1]
            results.append(result)
        return (jnp.concatenate(results, axis=0), state)

    _, pullback = jax.vjp(
        forward,
        inputs,
        step_logits[0],
        writer_full,
        reader_full,
        all_scores,
        log_rates,
        step_bias,
        skip_gain,
    )
    grads = pullback((upstream, end_pull.reshape(state_rows, heads, head_size)))
    score_grads = grads[4]
    reader_extra = jnp.einsum(
        "cts,csn->ctn", score_grads, writer_full.reshape(blocks, GROUP, state_rows), precision=HIGH
    ).reshape(tokens, state_rows)
    writer_extra = jnp.einsum(
        "cts,ctn->csn", score_grads, reader_full.reshape(blocks, GROUP, state_rows), precision=HIGH
    ).reshape(tokens, state_rows)
    factor = float(lax.axis_size("dp") * lax.axis_size("ctx") * tokens) ** (-0.5)
    head_terms = jnp.stack([grads[5], grads[6], grads[7]]) * factor
    devices = lax.axis_size("dp") * lax.axis_size("ctx")
    spread = jnp.broadcast_to(head_terms[None], (devices,) + head_terms.shape)
    head_total = jnp.sum(lax.all_to_all(spread, ("dp", "ctx"), 0, 0, tiled=True), axis=0)
    features_gradient = grads[0].reshape(tokens, width).astype(jnp.bfloat16)[None]
    return (
        features_gradient,
        grads[1][None],
        (grads[2] + writer_extra)[None],
        (grads[3] + reader_extra)[None],
        head_total,
    )


def solution(mesh):
    placed = (
        P("dp", "ctx", None),
        P("dp", None, "ctx"),
        P("dp", "ctx", None),
        P("dp", "ctx", None),
        P(),
        P(),
        P(),
        P("dp", None),
        P("dp", "ctx", None),
    )
    return jax.shard_map(
        shards,
        mesh=mesh,
        in_specs=placed,
        out_specs=(
            P("dp", "ctx", None),
            P("dp", None, "ctx"),
            P("dp", "ctx", None),
            P("dp", "ctx", None),
            P(),
        ),
        check_vma=False,
    )
```

```python
import jax
import jax.numpy as jnp
from jax import lax
from jax.experimental import pallas as pl
from jax.sharding import PartitionSpec as P

GROUP = 128


HIGH = lax.Precision.HIGHEST


def forward_kernel(moved_ref, decay_ref, out_ref):
    def step(j, state):
        out_ref[j] = state
        return decay_ref[j] * state + moved_ref[j]

    lax.fori_loop(0, moved_ref.shape[0], step, jnp.zeros(out_ref.shape[1:], jnp.float32))


def backward_kernel(moved_ref, decay_ref, out_ref):
    count = moved_ref.shape[0]

    def step(k, pull):
        j = count - 1 - k
        out_ref[j] = pull
        return decay_ref[j] * pull + moved_ref[j]

    lax.fori_loop(0, count, step, jnp.zeros(out_ref.shape[1:], jnp.float32))


def exchange_scan(through, local_state, local_pull, axis):
    count = lax.axis_size(axis)
    rows, width = local_state.shape
    heads = through.shape[0]
    half = count // 2
    part = rows // half
    sent = jnp.concatenate(
        [
            local_state.reshape(half, part, width),
            local_pull.reshape(half, part, width),
        ],
        axis=0,
    )
    spare = 128 * ((heads + 127) // 128)
    extra = jnp.zeros((count, part, spare), jnp.float32).at[:, 0, :heads].set(through[None, :])
    moved = lax.all_to_all(jnp.concatenate([sent, extra], axis=2), axis, 0, 0, tiled=True)
    decays = jnp.repeat(moved[:, 0, width : width + heads], width // heads, axis=1)[:, None, :]
    lanes = 512 if width % 512 == 0 else width

    def scan_with(kernel):
        return pl.pallas_call(
            kernel,
            out_shape=jax.ShapeDtypeStruct((count, part, width), jnp.float32),
            grid=(width // lanes,),
            in_specs=[
                pl.BlockSpec((count, part, lanes), lambda c: (0, 0, c)),
                pl.BlockSpec((count, 1, lanes), lambda c: (0, 0, c)),
            ],
            out_specs=pl.BlockSpec((count, part, lanes), lambda c: (0, 0, c)),
        )

    scanned = lax.cond(
        lax.axis_index(axis) < half,
        scan_with(forward_kernel),
        scan_with(backward_kernel),
        moved,
        decays,
    )
    back = lax.all_to_all(scanned, axis, 0, 0, tiled=True)
    return back[:half].reshape(rows, width), back[half:].reshape(rows, width)


def group_step(
    state,
    prior_segment,
    inputs,
    log_decay,
    step_size,
    scores,
    reader_piece,
    writer_piece,
    segment_piece,
    skip_gain,
):
    size = inputs.shape[0]
    cumulative = jnp.cumsum(log_decay, axis=1)
    causal = jnp.arange(size)[:, None] >= jnp.arange(size)[None, :]
    within = causal & (segment_piece[:, None] == segment_piece[None, :])
    spread = cumulative[:, :, None] - cumulative[:, None, :]
    decay = jnp.where(within[None], jnp.exp(jnp.where(within[None], spread, 0.0)), 0.0)
    weights = decay * scores[None] * step_size[:, None, :]
    inner = jnp.einsum("hts,shp->thp", weights, inputs, precision=HIGH)
    carry_in = jnp.where((segment_piece == prior_segment)[None], jnp.exp(cumulative), 0.0)
    rows, heads, head_size = state.shape
    from_state = (
        jnp.dot(reader_piece, state.reshape(rows, heads * head_size), precision=HIGH).reshape(
            size, heads, head_size
        )
        * carry_in.T[:, :, None]
    )
    result = inner + from_state + skip_gain[None, :, None] * inputs
    to_end = (
        jnp.where(
            (segment_piece == segment_piece[-1])[None],
            jnp.exp(cumulative[:, -1:] - cumulative),
            0.0,
        )
        * step_size
    )
    fresh = jnp.dot(
        writer_piece.T, (to_end.T[:, :, None] * inputs).reshape(size, heads * head_size), precision=HIGH
    ).reshape(rows, heads, head_size)
    new_state = carry_in[:, -1][None, :, None] * state + fresh
    return (result, new_state)


def shards(
    features,
    step_logits,
    writer,
    reader,
    log_rates,
    step_bias,
    skip_gain,
    document_lengths,
    cotangent,
):
    tokens = features.shape[1]
    width = features.shape[2]
    heads = log_rates.shape[0]
    head_size = width // heads
    state_rows = writer.shape[2]
    blocks = tokens // GROUP
    position = lax.axis_index("ctx") * tokens + jnp.arange(tokens, dtype=jnp.int32)
    starts = jnp.cumsum(document_lengths[0])[:-1]
    segment = jnp.sum(position[:, None] >= starts[None, :], axis=1)
    prior_segment = jnp.sum(position[0] - 1 >= starts)
    inputs = features[0].astype(jnp.float32).reshape(tokens, heads, head_size)
    writer_full = writer[0].astype(jnp.float32)
    reader_full = reader[0].astype(jnp.float32)
    upstream = cotangent[0].astype(jnp.float32).reshape(tokens, heads, head_size)
    all_scores = jnp.einsum(
        "ctn,csn->cts",
        reader[0].reshape(blocks, GROUP, state_rows),
        writer[0].reshape(blocks, GROUP, state_rows),
        preferred_element_type=jnp.float32,
    )
    step_size = jax.nn.softplus(step_logits[0] + step_bias[:, None])
    log_decay = -jnp.exp(log_rates)[:, None] * step_size
    cumulative = jnp.cumsum(log_decay, axis=1)
    from_start = jnp.where((segment == prior_segment)[None], jnp.exp(cumulative), 0.0)
    through = from_start[:, -1]
    to_end = (
        jnp.where((segment == segment[-1])[None], jnp.exp(cumulative[:, -1:] - cumulative), 0.0)
        * step_size
    )
    local_state = jnp.dot(
        writer_full.T, (to_end.T[:, :, None] * inputs).reshape(tokens, width), precision=HIGH
    )
    local_pull = jnp.dot(
        reader_full.T, (from_start.T[:, :, None] * upstream).reshape(tokens, width), precision=HIGH
    )
    start_state, end_pull = exchange_scan(through, local_state, local_pull, "ctx")
    stepper = group_step

    def forward(inputs_in, logits, writer_in, reader_in, scores_in, rates, bias, gain):
        sizes_in = jax.nn.softplus(logits + bias[:, None])
        decays_in = -jnp.exp(rates)[:, None] * sizes_in
        state = start_state.reshape(state_rows, heads, head_size)
        prior = prior_segment
        results = []
        for number in range(blocks):
            first = number * GROUP
            final = first + GROUP
            result, state = stepper(
                state,
                prior,
                inputs_in[first:final],
                decays_in[:, first:final],
                sizes_in[:, first:final],
                scores_in[number],
                reader_in[first:final],
                writer_in[first:final],
                segment[first:final],
                gain,
            )
            prior = segment[final - 1]
            results.append(result)
        return (jnp.concatenate(results, axis=0), state)

    _, pullback = jax.vjp(
        forward,
        inputs,
        step_logits[0],
        writer_full,
        reader_full,
        all_scores,
        log_rates,
        step_bias,
        skip_gain,
    )
    grads = pullback((upstream, end_pull.reshape(state_rows, heads, head_size)))
    score_grads = grads[4]
    reader_extra = jnp.einsum(
        "cts,csn->ctn", score_grads, writer_full.reshape(blocks, GROUP, state_rows), precision=HIGH
    ).reshape(tokens, state_rows)
    writer_extra = jnp.einsum(
        "cts,ctn->csn", score_grads, reader_full.reshape(blocks, GROUP, state_rows), precision=HIGH
    ).reshape(tokens, state_rows)
    factor = float(lax.axis_size("dp") * lax.axis_size("ctx") * tokens) ** (-0.5)
    head_terms = jnp.stack([grads[5], grads[6], grads[7]]) * factor
    devices = lax.axis_size("dp") * lax.axis_size("ctx")
    spread = jnp.broadcast_to(head_terms[None], (devices,) + head_terms.shape)
    head_total = jnp.sum(lax.all_to_all(spread, ("dp", "ctx"), 0, 0, tiled=True), axis=0)
    features_gradient = grads[0].reshape(tokens, width).astype(jnp.bfloat16)[None]
    return (
        features_gradient,
        grads[1][None],
        (grads[2] + writer_extra)[None],
        (grads[3] + reader_extra)[None],
        head_total,
    )


def solution(mesh):
    placed = (
        P("dp", "ctx", None),
        P("dp", None, "ctx"),
        P("dp", "ctx", None),
        P("dp", "ctx", None),
        P(),
        P(),
        P(),
        P("dp", None),
        P("dp", "ctx", None),
    )
    return jax.shard_map(
        shards,
        mesh=mesh,
        in_specs=placed,
        out_specs=(
            P("dp", "ctx", None),
            P("dp", None, "ctx"),
            P("dp", "ctx", None),
            P("dp", "ctx", None),
            P(),
        ),
        check_vma=False,
    )
```

```python
import jax
import jax.numpy as jnp
from jax import lax
from jax.experimental import pallas as pl
from jax.sharding import PartitionSpec as P

GROUP = 128


HIGH = lax.Precision.HIGHEST


def forward_kernel(moved_ref, decay_ref, out_ref):
    def step(j, state):
        out_ref[j] = state
        return decay_ref[j] * state + moved_ref[j]

    lax.fori_loop(0, moved_ref.shape[0], step, jnp.zeros(out_ref.shape[1:], jnp.float32))


def backward_kernel(moved_ref, decay_ref, out_ref):
    count = moved_ref.shape[0]

    def step(k, pull):
        j = count - 1 - k
        out_ref[j] = pull
        return decay_ref[j] * pull + moved_ref[j]

    lax.fori_loop(0, count, step, jnp.zeros(out_ref.shape[1:], jnp.float32))


def exchange_scan(through, local_state, local_pull, axis):
    count = lax.axis_size(axis)
    rows, width = local_state.shape
    heads = through.shape[0]
    half = count // 2
    part = rows // half
    sent = jnp.concatenate(
        [
            local_state.reshape(half, part, width),
            local_pull.reshape(half, part, width),
        ],
        axis=0,
    )
    spare = 128 * ((heads + 127) // 128)
    extra = jnp.zeros((count, part, spare), jnp.float32).at[:, 0, :heads].set(through[None, :])
    moved = lax.all_to_all(jnp.concatenate([sent, extra], axis=2), axis, 0, 0, tiled=True)
    decays = jnp.repeat(moved[:, 0, width : width + heads], width // heads, axis=1)[:, None, :]
    lanes = 512 if width % 512 == 0 else width

    def scan_with(kernel):
        return pl.pallas_call(
            kernel,
            out_shape=jax.ShapeDtypeStruct((count, part, width), jnp.float32),
            grid=(width // lanes,),
            in_specs=[
                pl.BlockSpec((count, part, lanes), lambda c: (0, 0, c)),
                pl.BlockSpec((count, 1, lanes), lambda c: (0, 0, c)),
            ],
            out_specs=pl.BlockSpec((count, part, lanes), lambda c: (0, 0, c)),
        )

    scanned = lax.cond(
        lax.axis_index(axis) < half,
        scan_with(forward_kernel),
        scan_with(backward_kernel),
        moved,
        decays,
    )
    back = lax.all_to_all(scanned, axis, 0, 0, tiled=True)
    return back[:half].reshape(rows, width), back[half:].reshape(rows, width)


def group_step(
    state,
    prior_segment,
    inputs,
    log_decay,
    step_size,
    scores,
    reader_piece,
    writer_piece,
    segment_piece,
    skip_gain,
):
    size = inputs.shape[0]
    cumulative = jnp.cumsum(log_decay, axis=1)
    causal = jnp.arange(size)[:, None] >= jnp.arange(size)[None, :]
    within = causal & (segment_piece[:, None] == segment_piece[None, :])
    spread = cumulative[:, :, None] - cumulative[:, None, :]
    decay = jnp.where(within[None], jnp.exp(jnp.where(within[None], spread, 0.0)), 0.0)
    weights = decay * scores[None] * step_size[:, None, :]
    inner = jnp.einsum("hts,shp->thp", weights, inputs, precision=HIGH)
    carry_in = jnp.where((segment_piece == prior_segment)[None], jnp.exp(cumulative), 0.0)
    rows, heads, head_size = state.shape
    from_state = (
        jnp.dot(reader_piece, state.reshape(rows, heads * head_size), precision=HIGH).reshape(
            size, heads, head_size
        )
        * carry_in.T[:, :, None]
    )
    result = inner + from_state + skip_gain[None, :, None] * inputs
    to_end = (
        jnp.where(
            (segment_piece == segment_piece[-1])[None],
            jnp.exp(cumulative[:, -1:] - cumulative),
            0.0,
        )
        * step_size
    )
    fresh = jnp.dot(
        writer_piece.T, (to_end.T[:, :, None] * inputs).reshape(size, heads * head_size), precision=HIGH
    ).reshape(rows, heads, head_size)
    new_state = carry_in[:, -1][None, :, None] * state + fresh
    return (result, new_state)


def shards(
    features,
    step_logits,
    writer,
    reader,
    log_rates,
    step_bias,
    skip_gain,
    document_lengths,
    cotangent,
):
    tokens = features.shape[1]
    width = features.shape[2]
    heads = log_rates.shape[0]
    head_size = width // heads
    state_rows = writer.shape[2]
    blocks = tokens // GROUP
    position = lax.axis_index("ctx") * tokens + jnp.arange(tokens, dtype=jnp.int32)
    starts = jnp.cumsum(document_lengths[0])[:-1]
    segment = jnp.sum(position[:, None] >= starts[None, :], axis=1)
    prior_segment = jnp.sum(position[0] - 1 >= starts)
    inputs = features[0].astype(jnp.float32).reshape(tokens, heads, head_size)
    writer_full = writer[0].astype(jnp.float32)
    reader_full = reader[0].astype(jnp.float32)
    upstream = cotangent[0].astype(jnp.float32).reshape(tokens, heads, head_size)
    all_scores = jnp.einsum(
        "ctn,csn->cts",
        reader[0].reshape(blocks, GROUP, state_rows),
        writer[0].reshape(blocks, GROUP, state_rows),
        preferred_element_type=jnp.float32,
    )
    step_size = jax.nn.softplus(step_logits[0] + step_bias[:, None])
    log_decay = -jnp.exp(log_rates)[:, None] * step_size
    cumulative = jnp.cumsum(log_decay, axis=1)
    from_start = jnp.where((segment == prior_segment)[None], jnp.exp(cumulative), 0.0)
    through = from_start[:, -1]
    to_end = (
        jnp.where((segment == segment[-1])[None], jnp.exp(cumulative[:, -1:] - cumulative), 0.0)
        * step_size
    )
    local_state = jnp.dot(
        writer_full.T, (to_end.T[:, :, None] * inputs).reshape(tokens, width), precision=HIGH
    )
    local_pull = jnp.dot(
        reader_full.T, (from_start.T[:, :, None] * upstream).reshape(tokens, width), precision=HIGH
    )
    start_state, end_pull = exchange_scan(through, local_state, local_pull, "ctx")
    stepper = group_step

    def forward(inputs_in, logits, writer_in, reader_in, scores_in, rates, bias, gain):
        sizes_in = jax.nn.softplus(logits + bias[:, None])
        decays_in = -jnp.exp(rates)[:, None] * sizes_in
        state = start_state.reshape(state_rows, heads, head_size)
        prior = prior_segment
        results = []
        for number in range(blocks):
            first = number * GROUP
            final = first + GROUP
            result, state = stepper(
                state,
                prior,
                inputs_in[first:final],
                decays_in[:, first:final],
                sizes_in[:, first:final],
                scores_in[number],
                reader_in[first:final],
                writer_in[first:final],
                segment[first:final],
                gain,
            )
            prior = segment[final - 1]
            results.append(result)
        return (jnp.concatenate(results, axis=0), state)

    _, pullback = jax.vjp(
        forward,
        inputs,
        step_logits[0],
        writer_full,
        reader_full,
        all_scores,
        log_rates,
        step_bias,
        skip_gain,
    )
    grads = pullback((upstream, end_pull.reshape(state_rows, heads, head_size)))
    score_grads = grads[4]
    reader_extra = jnp.einsum(
        "cts,csn->ctn", score_grads, writer_full.reshape(blocks, GROUP, state_rows), precision=HIGH
    ).reshape(tokens, state_rows)
    writer_extra = jnp.einsum(
        "cts,ctn->csn", score_grads, reader_full.reshape(blocks, GROUP, state_rows), precision=HIGH
    ).reshape(tokens, state_rows)
    factor = float(lax.axis_size("dp") * lax.axis_size("ctx") * tokens) ** (-0.5)
    head_terms = jnp.stack([grads[5], grads[6], grads[7]]) * factor
    devices = lax.axis_size("dp") * lax.axis_size("ctx")
    flat = head_terms.reshape(-1)
    lanes = 128 * ((flat.shape[0] + 127) // 128)
    spread = jnp.broadcast_to(jnp.pad(flat, (0, lanes - flat.shape[0]))[None], (devices, lanes))
    summed = jnp.sum(lax.all_to_all(spread, ("dp", "ctx"), 0, 0, tiled=True), axis=0)
    head_total = summed[: flat.shape[0]].reshape(head_terms.shape)
    features_gradient = grads[0].reshape(tokens, width).astype(jnp.bfloat16)[None]
    return (
        features_gradient,
        grads[1][None],
        (grads[2] + writer_extra)[None],
        (grads[3] + reader_extra)[None],
        head_total,
    )


def solution(mesh):
    placed = (
        P("dp", "ctx", None),
        P("dp", None, "ctx"),
        P("dp", "ctx", None),
        P("dp", "ctx", None),
        P(),
        P(),
        P(),
        P("dp", None),
        P("dp", "ctx", None),
    )
    return jax.shard_map(
        shards,
        mesh=mesh,
        in_specs=placed,
        out_specs=(
            P("dp", "ctx", None),
            P("dp", None, "ctx"),
            P("dp", "ctx", None),
            P("dp", "ctx", None),
            P(),
        ),
        check_vma=False,
    )
```

```python
import jax
import jax.numpy as jnp
from jax import lax
from jax.experimental import pallas as pl
from jax.sharding import PartitionSpec as P

SPAN = 256


HIGH = lax.Precision.HIGHEST


def forward_kernel(moved_ref, decay_ref, out_ref):
    def step(j, state):
        out_ref[j] = state
        return decay_ref[j] * state + moved_ref[j]

    lax.fori_loop(0, moved_ref.shape[0], step, jnp.zeros(out_ref.shape[1:], jnp.float32))


def backward_kernel(moved_ref, decay_ref, out_ref):
    count = moved_ref.shape[0]

    def step(k, pull):
        j = count - 1 - k
        out_ref[j] = pull
        return decay_ref[j] * pull + moved_ref[j]

    lax.fori_loop(0, count, step, jnp.zeros(out_ref.shape[1:], jnp.float32))


def exchange_scan(through, local_state, local_pull, axis):
    count = lax.axis_size(axis)
    rows, width = local_state.shape
    heads = through.shape[0]
    half = count // 2
    part = rows // half
    sent = jnp.concatenate(
        [
            local_state.reshape(half, part, width),
            local_pull.reshape(half, part, width),
        ],
        axis=0,
    )
    spare = 128 * ((heads + 127) // 128)
    extra = jnp.zeros((count, part, spare), jnp.float32).at[:, 0, :heads].set(through[None, :])
    moved = lax.all_to_all(jnp.concatenate([sent, extra], axis=2), axis, 0, 0, tiled=True)
    decays = jnp.repeat(moved[:, 0, width : width + heads], width // heads, axis=1)[:, None, :]
    lanes = 512 if width % 512 == 0 else width

    def scan_with(kernel):
        return pl.pallas_call(
            kernel,
            out_shape=jax.ShapeDtypeStruct((count, part, width), jnp.float32),
            grid=(width // lanes,),
            in_specs=[
                pl.BlockSpec((count, part, lanes), lambda c: (0, 0, c)),
                pl.BlockSpec((count, 1, lanes), lambda c: (0, 0, c)),
            ],
            out_specs=pl.BlockSpec((count, part, lanes), lambda c: (0, 0, c)),
        )

    scanned = lax.cond(
        lax.axis_index(axis) < half,
        scan_with(forward_kernel),
        scan_with(backward_kernel),
        moved,
        decays,
    )
    back = lax.all_to_all(scanned, axis, 0, 0, tiled=True)
    return back[:half].reshape(rows, width), back[half:].reshape(rows, width)


def group_step(
    state,
    prior_segment,
    inputs,
    log_decay,
    step_size,
    scores,
    reader_piece,
    writer_piece,
    segment_piece,
    skip_gain,
):
    size = inputs.shape[0]
    cumulative = jnp.cumsum(log_decay, axis=1)
    causal = jnp.arange(size)[:, None] >= jnp.arange(size)[None, :]
    within = causal & (segment_piece[:, None] == segment_piece[None, :])
    spread = cumulative[:, :, None] - cumulative[:, None, :]
    decay = jnp.where(within[None], jnp.exp(jnp.where(within[None], spread, 0.0)), 0.0)
    weights = decay * scores[None] * step_size[:, None, :]
    inner = jnp.einsum("hts,shp->thp", weights, inputs, precision=HIGH)
    carry_in = jnp.where((segment_piece == prior_segment)[None], jnp.exp(cumulative), 0.0)
    rows, heads, head_size = state.shape
    from_state = (
        jnp.dot(reader_piece, state.reshape(rows, heads * head_size), precision=HIGH).reshape(
            size, heads, head_size
        )
        * carry_in.T[:, :, None]
    )
    result = inner + from_state + skip_gain[None, :, None] * inputs
    to_end = (
        jnp.where(
            (segment_piece == segment_piece[-1])[None],
            jnp.exp(cumulative[:, -1:] - cumulative),
            0.0,
        )
        * step_size
    )
    fresh = jnp.dot(
        writer_piece.T, (to_end.T[:, :, None] * inputs).reshape(size, heads * head_size), precision=HIGH
    ).reshape(rows, heads, head_size)
    new_state = carry_in[:, -1][None, :, None] * state + fresh
    return (result, new_state)


def shards(
    features,
    step_logits,
    writer,
    reader,
    log_rates,
    step_bias,
    skip_gain,
    document_lengths,
    cotangent,
):
    tokens = features.shape[1]
    width = features.shape[2]
    heads = log_rates.shape[0]
    head_size = width // heads
    state_rows = writer.shape[2]
    span = min(SPAN, tokens)
    blocks = tokens // span
    position = lax.axis_index("ctx") * tokens + jnp.arange(tokens, dtype=jnp.int32)
    starts = jnp.cumsum(document_lengths[0])[:-1]
    segment = jnp.sum(position[:, None] >= starts[None, :], axis=1)
    prior_segment = jnp.sum(position[0] - 1 >= starts)
    inputs = features[0].astype(jnp.float32).reshape(tokens, heads, head_size)
    writer_full = writer[0].astype(jnp.float32)
    reader_full = reader[0].astype(jnp.float32)
    upstream = cotangent[0].astype(jnp.float32).reshape(tokens, heads, head_size)
    all_scores = jnp.einsum(
        "ctn,csn->cts",
        reader[0].reshape(blocks, span, state_rows),
        writer[0].reshape(blocks, span, state_rows),
        preferred_element_type=jnp.float32,
    )
    step_size = jax.nn.softplus(step_logits[0] + step_bias[:, None])
    log_decay = -jnp.exp(log_rates)[:, None] * step_size
    cumulative = jnp.cumsum(log_decay, axis=1)
    from_start = jnp.where((segment == prior_segment)[None], jnp.exp(cumulative), 0.0)
    through = from_start[:, -1]
    to_end = (
        jnp.where((segment == segment[-1])[None], jnp.exp(cumulative[:, -1:] - cumulative), 0.0)
        * step_size
    )
    local_state = jnp.dot(
        writer_full.T, (to_end.T[:, :, None] * inputs).reshape(tokens, width), precision=HIGH
    )
    local_pull = jnp.dot(
        reader_full.T, (from_start.T[:, :, None] * upstream).reshape(tokens, width), precision=HIGH
    )
    start_state, end_pull = exchange_scan(through, local_state, local_pull, "ctx")
    stepper = group_step

    def forward(inputs_in, logits, writer_in, reader_in, scores_in, rates, bias, gain):
        sizes_in = jax.nn.softplus(logits + bias[:, None])
        decays_in = -jnp.exp(rates)[:, None] * sizes_in
        state = start_state.reshape(state_rows, heads, head_size)
        prior = prior_segment
        results = []
        for number in range(blocks):
            first = number * span
            final = first + span
            result, state = stepper(
                state,
                prior,
                inputs_in[first:final],
                decays_in[:, first:final],
                sizes_in[:, first:final],
                scores_in[number],
                reader_in[first:final],
                writer_in[first:final],
                segment[first:final],
                gain,
            )
            prior = segment[final - 1]
            results.append(result)
        return (jnp.concatenate(results, axis=0), state)

    _, pullback = jax.vjp(
        forward,
        inputs,
        step_logits[0],
        writer_full,
        reader_full,
        all_scores,
        log_rates,
        step_bias,
        skip_gain,
    )
    grads = pullback((upstream, end_pull.reshape(state_rows, heads, head_size)))
    score_grads = grads[4]
    reader_extra = jnp.einsum(
        "cts,csn->ctn", score_grads, writer_full.reshape(blocks, span, state_rows), precision=HIGH
    ).reshape(tokens, state_rows)
    writer_extra = jnp.einsum(
        "cts,ctn->csn", score_grads, reader_full.reshape(blocks, span, state_rows), precision=HIGH
    ).reshape(tokens, state_rows)
    factor = float(lax.axis_size("dp") * lax.axis_size("ctx") * tokens) ** (-0.5)
    head_terms = jnp.stack([grads[5], grads[6], grads[7]]) * factor
    devices = lax.axis_size("dp") * lax.axis_size("ctx")
    flat = head_terms.reshape(-1)
    lanes = 128 * ((flat.shape[0] + 127) // 128)
    spread = jnp.broadcast_to(jnp.pad(flat, (0, lanes - flat.shape[0]))[None], (devices, lanes))
    summed = jnp.sum(lax.all_to_all(spread, ("dp", "ctx"), 0, 0, tiled=True), axis=0)
    head_total = summed[: flat.shape[0]].reshape(head_terms.shape)
    features_gradient = grads[0].reshape(tokens, width).astype(jnp.bfloat16)[None]
    return (
        features_gradient,
        grads[1][None],
        (grads[2] + writer_extra)[None],
        (grads[3] + reader_extra)[None],
        head_total,
    )


def solution(mesh):
    placed = (
        P("dp", "ctx", None),
        P("dp", None, "ctx"),
        P("dp", "ctx", None),
        P("dp", "ctx", None),
        P(),
        P(),
        P(),
        P("dp", None),
        P("dp", "ctx", None),
    )
    return jax.shard_map(
        shards,
        mesh=mesh,
        in_specs=placed,
        out_specs=(
            P("dp", "ctx", None),
            P("dp", None, "ctx"),
            P("dp", "ctx", None),
            P("dp", "ctx", None),
            P(),
        ),
        check_vma=False,
    )
```

```python
import jax
import jax.numpy as jnp
from jax import lax
from jax.experimental import pallas as pl
from jax.sharding import PartitionSpec as P

SPAN = 256


HIGH = lax.Precision.HIGH


def forward_kernel(moved_ref, decay_ref, out_ref):
    def step(j, state):
        out_ref[j] = state
        return decay_ref[j] * state + moved_ref[j]

    lax.fori_loop(0, moved_ref.shape[0], step, jnp.zeros(out_ref.shape[1:], jnp.float32))


def backward_kernel(moved_ref, decay_ref, out_ref):
    count = moved_ref.shape[0]

    def step(k, pull):
        j = count - 1 - k
        out_ref[j] = pull
        return decay_ref[j] * pull + moved_ref[j]

    lax.fori_loop(0, count, step, jnp.zeros(out_ref.shape[1:], jnp.float32))


def exchange_scan(through, local_state, local_pull, axis):
    count = lax.axis_size(axis)
    rows, width = local_state.shape
    heads = through.shape[0]
    half = count // 2
    part = rows // half
    sent = jnp.concatenate(
        [
            local_state.reshape(half, part, width),
            local_pull.reshape(half, part, width),
        ],
        axis=0,
    )
    spare = 128 * ((heads + 127) // 128)
    extra = jnp.zeros((count, part, spare), jnp.float32).at[:, 0, :heads].set(through[None, :])
    moved = lax.all_to_all(jnp.concatenate([sent, extra], axis=2), axis, 0, 0, tiled=True)
    decays = jnp.repeat(moved[:, 0, width : width + heads], width // heads, axis=1)[:, None, :]
    lanes = 512 if width % 512 == 0 else width

    def scan_with(kernel):
        return pl.pallas_call(
            kernel,
            out_shape=jax.ShapeDtypeStruct((count, part, width), jnp.float32),
            grid=(width // lanes,),
            in_specs=[
                pl.BlockSpec((count, part, lanes), lambda c: (0, 0, c)),
                pl.BlockSpec((count, 1, lanes), lambda c: (0, 0, c)),
            ],
            out_specs=pl.BlockSpec((count, part, lanes), lambda c: (0, 0, c)),
        )

    scanned = lax.cond(
        lax.axis_index(axis) < half,
        scan_with(forward_kernel),
        scan_with(backward_kernel),
        moved,
        decays,
    )
    back = lax.all_to_all(scanned, axis, 0, 0, tiled=True)
    return back[:half].reshape(rows, width), back[half:].reshape(rows, width)


def group_step(
    state,
    prior_segment,
    inputs,
    log_decay,
    step_size,
    scores,
    reader_piece,
    writer_piece,
    segment_piece,
    skip_gain,
):
    size = inputs.shape[0]
    cumulative = jnp.cumsum(log_decay, axis=1)
    causal = jnp.arange(size)[:, None] >= jnp.arange(size)[None, :]
    within = causal & (segment_piece[:, None] == segment_piece[None, :])
    spread = cumulative[:, :, None] - cumulative[:, None, :]
    decay = jnp.where(within[None], jnp.exp(jnp.where(within[None], spread, 0.0)), 0.0)
    weights = decay * scores[None] * step_size[:, None, :]
    inner = jnp.einsum("hts,shp->thp", weights, inputs, precision=HIGH)
    carry_in = jnp.where((segment_piece == prior_segment)[None], jnp.exp(cumulative), 0.0)
    rows, heads, head_size = state.shape
    from_state = (
        jnp.dot(reader_piece, state.reshape(rows, heads * head_size), precision=HIGH).reshape(
            size, heads, head_size
        )
        * carry_in.T[:, :, None]
    )
    result = inner + from_state + skip_gain[None, :, None] * inputs
    to_end = (
        jnp.where(
            (segment_piece == segment_piece[-1])[None],
            jnp.exp(cumulative[:, -1:] - cumulative),
            0.0,
        )
        * step_size
    )
    fresh = jnp.dot(
        writer_piece.T, (to_end.T[:, :, None] * inputs).reshape(size, heads * head_size), precision=HIGH
    ).reshape(rows, heads, head_size)
    new_state = carry_in[:, -1][None, :, None] * state + fresh
    return (result, new_state)


def shards(
    features,
    step_logits,
    writer,
    reader,
    log_rates,
    step_bias,
    skip_gain,
    document_lengths,
    cotangent,
):
    tokens = features.shape[1]
    width = features.shape[2]
    heads = log_rates.shape[0]
    head_size = width // heads
    state_rows = writer.shape[2]
    span = min(SPAN, tokens)
    blocks = tokens // span
    position = lax.axis_index("ctx") * tokens + jnp.arange(tokens, dtype=jnp.int32)
    starts = jnp.cumsum(document_lengths[0])[:-1]
    segment = jnp.sum(position[:, None] >= starts[None, :], axis=1)
    prior_segment = jnp.sum(position[0] - 1 >= starts)
    inputs = features[0].astype(jnp.float32).reshape(tokens, heads, head_size)
    writer_full = writer[0].astype(jnp.float32)
    reader_full = reader[0].astype(jnp.float32)
    upstream = cotangent[0].astype(jnp.float32).reshape(tokens, heads, head_size)
    all_scores = jnp.einsum(
        "ctn,csn->cts",
        reader[0].reshape(blocks, span, state_rows),
        writer[0].reshape(blocks, span, state_rows),
        preferred_element_type=jnp.float32,
    )
    step_size = jax.nn.softplus(step_logits[0] + step_bias[:, None])
    log_decay = -jnp.exp(log_rates)[:, None] * step_size
    cumulative = jnp.cumsum(log_decay, axis=1)
    from_start = jnp.where((segment == prior_segment)[None], jnp.exp(cumulative), 0.0)
    through = from_start[:, -1]
    to_end = (
        jnp.where((segment == segment[-1])[None], jnp.exp(cumulative[:, -1:] - cumulative), 0.0)
        * step_size
    )
    local_state = jnp.dot(
        writer_full.T, (to_end.T[:, :, None] * inputs).reshape(tokens, width), precision=HIGH
    )
    local_pull = jnp.dot(
        reader_full.T, (from_start.T[:, :, None] * upstream).reshape(tokens, width), precision=HIGH
    )
    start_state, end_pull = exchange_scan(through, local_state, local_pull, "ctx")
    stepper = group_step

    def forward(inputs_in, logits, writer_in, reader_in, scores_in, rates, bias, gain):
        sizes_in = jax.nn.softplus(logits + bias[:, None])
        decays_in = -jnp.exp(rates)[:, None] * sizes_in
        state = start_state.reshape(state_rows, heads, head_size)
        prior = prior_segment
        results = []
        for number in range(blocks):
            first = number * span
            final = first + span
            result, state = stepper(
                state,
                prior,
                inputs_in[first:final],
                decays_in[:, first:final],
                sizes_in[:, first:final],
                scores_in[number],
                reader_in[first:final],
                writer_in[first:final],
                segment[first:final],
                gain,
            )
            prior = segment[final - 1]
            results.append(result)
        return (jnp.concatenate(results, axis=0), state)

    _, pullback = jax.vjp(
        forward,
        inputs,
        step_logits[0],
        writer_full,
        reader_full,
        all_scores,
        log_rates,
        step_bias,
        skip_gain,
    )
    grads = pullback((upstream, end_pull.reshape(state_rows, heads, head_size)))
    score_grads = grads[4]
    reader_extra = jnp.einsum(
        "cts,csn->ctn", score_grads, writer_full.reshape(blocks, span, state_rows), precision=HIGH
    ).reshape(tokens, state_rows)
    writer_extra = jnp.einsum(
        "cts,ctn->csn", score_grads, reader_full.reshape(blocks, span, state_rows), precision=HIGH
    ).reshape(tokens, state_rows)
    factor = float(lax.axis_size("dp") * lax.axis_size("ctx") * tokens) ** (-0.5)
    head_terms = jnp.stack([grads[5], grads[6], grads[7]]) * factor
    devices = lax.axis_size("dp") * lax.axis_size("ctx")
    flat = head_terms.reshape(-1)
    lanes = 128 * ((flat.shape[0] + 127) // 128)
    spread = jnp.broadcast_to(jnp.pad(flat, (0, lanes - flat.shape[0]))[None], (devices, lanes))
    summed = jnp.sum(lax.all_to_all(spread, ("dp", "ctx"), 0, 0, tiled=True), axis=0)
    head_total = summed[: flat.shape[0]].reshape(head_terms.shape)
    features_gradient = grads[0].reshape(tokens, width).astype(jnp.bfloat16)[None]
    return (
        features_gradient,
        grads[1][None],
        (grads[2] + writer_extra)[None],
        (grads[3] + reader_extra)[None],
        head_total,
    )


def solution(mesh):
    placed = (
        P("dp", "ctx", None),
        P("dp", None, "ctx"),
        P("dp", "ctx", None),
        P("dp", "ctx", None),
        P(),
        P(),
        P(),
        P("dp", None),
        P("dp", "ctx", None),
    )
    return jax.shard_map(
        shards,
        mesh=mesh,
        in_specs=placed,
        out_specs=(
            P("dp", "ctx", None),
            P("dp", None, "ctx"),
            P("dp", "ctx", None),
            P("dp", "ctx", None),
            P(),
        ),
        check_vma=False,
    )
```
